512 devices in a mesh: island: 16 (over z, x_hi), fsdp: 32 (over y, x_lo, core).
Axes of the slice: x: 4 (x_hi: 2, x_lo: 2; x = x_hi * 2 + x_lo), y: 8, z: 8, core: 2. Of those that a mesh axis runs over, the one named last changes fastest.
Arguments:
- block_input: bfloat16 [65536, 8192], P(('island', 'fsdp')), may hold values from -170 to 170
- lang_ids: int32 [65536], P(('island', 'fsdp')), may hold values from 0 to 15
- queries: bfloat16 [65536, 4096], P(('island', 'fsdp')), may hold values from -52 to 52
- saved_keys: bfloat16 [65536, 512], P(('island', 'fsdp')), may hold values from -4 to 4
- out_grad: bfloat16 [65536, 4096], P(('island', 'fsdp')), may hold values from -70 to 70
- local_wv: bfloat16 [16, 8192, 512], P('island', 'fsdp'), may hold values from -8 to 8
- local_gain: bfloat16 [16, 16, 8192], P('island'), may hold values from -3 to 5
- outer_wv: float32 [8192, 512], P('fsdp', 'island'), may hold values from -4 to 4
- wv_momentum: float32 [8192, 512], P('fsdp', 'island'), may hold values from -1.8 to 1.8
- outer_gain: float32 [16, 8192], P('island', 'fsdp'), may hold values from 0.5 to 1.5
- gain_momentum: float32 [16, 8192], P('island', 'fsdp'), may hold values from -1.8 to 1.8
Outputs:
- new_outer_wv: float32 [8192, 512], P('fsdp', 'island')
- new_wv_momentum: float32 [8192, 512], P('fsdp', 'island')
- new_outer_gain: float32 [16, 8192], P('island', 'fsdp')
- new_gain_momentum: float32 [16, 8192], P('island', 'fsdp')
The draws below stay inside these ranges and needn't reach their ends.
All inputs are finite; a program needn't handle non-finite values.
Results may differ from the reference program's by a relative error of at most 0.00045.
Values may be sent and summed in bfloat16 or wider, within the bound.
No kernel may reach another device: no remote copies, remote signals or barrier semaphores. Data moves between devices by JAX's collectives and lax.ppermute only.
A program may use at most 64 MiB of HBM per device.

```python
import math
import jax
import jax.numpy as jnp
from jax import lax

D = 8192
HEADS = 32
KV_HEADS = 4
HEAD_DIM = 128
LANGS = 16
SEQ_LEN = 128
TOK_DEV = 128
TOKENS = 65536
KV_WIDTH = 512
N_ISLAND = 16
N_FSDP = 32


def rough(key, shape):
    return jnp.clip(jax.random.normal(key, shape, jnp.float32), -4.0, 4.0)


def key_rows(key):
    base = rough(jax.random.fold_in(key, 31), (TOKENS, KV_HEADS * HEAD_DIM))
    return base


def draw_saved_keys(key, part):
    return key_rows(key).astype(jnp.bfloat16)


def draw_queries(key, part):
    base = rough(jax.random.fold_in(key, 32), (TOKENS, HEADS * HEAD_DIM))
    return base.astype(jnp.bfloat16)


def sequence_shared(key, width):
    shared = rough(key, (TOKENS // SEQ_LEN, width))
    return jnp.repeat(shared, SEQ_LEN, axis=0)


def draw_block_input(key, part):
    column_scale = jnp.exp(jax.random.uniform(jax.random.fold_in(key, 1), (D,), jnp.float32, 0.0, math.log(10.0)))
    column_scale = column_scale * (1.0 + 2.0 * jnp.arange(D, dtype=jnp.float32) / D)
    base = rough(jax.random.fold_in(key, 2), (TOKENS, D))
    shared = sequence_shared(jax.random.fold_in(key, 5), D)
    mixed = 0.75 * base + 0.6 * shared
    return (mixed * column_scale[None, :]).astype(jnp.bfloat16)


def draw_out_grad(key, part):
    span = TOK_DEV * N_FSDP
    ramp = 1.0 + 2.0 * (jnp.arange(TOKENS, dtype=jnp.int32) % span).astype(jnp.float32) / span
    row_scale = jnp.exp(jax.random.uniform(jax.random.fold_in(key, 3), (TOKENS,), jnp.float32, 0.0, math.log(5.0))) * ramp
    base = rough(jax.random.fold_in(key, 4), (TOKENS, HEADS * HEAD_DIM))
    shared = sequence_shared(jax.random.fold_in(key, 6), HEADS * HEAD_DIM)
    mixed = 0.75 * base + 0.4 * shared
    return (mixed * row_scale[:, None]).astype(jnp.bfloat16)


def wv_parts(key):
    shape = (D, KV_HEADS * HEAD_DIM)
    outer = rough(jax.random.fold_in(key, 41), shape)
    common = rough(jax.random.fold_in(key, 42), shape)
    own = rough(jax.random.fold_in(key, 43), (N_ISLAND,) + shape)
    ramp = 0.15 * (1.0 + 2.0 * jnp.arange(N_ISLAND, dtype=jnp.float32) / max(N_ISLAND - 1, 1))
    local = outer[None] - ramp.reshape(-1, 1, 1) * (common[None] + own)
    return (outer, local)


def draw_outer_wv(key, part):
    return wv_parts(key)[0]


def draw_local_wv(key, part):
    return wv_parts(key)[1].astype(jnp.bfloat16)


def gain_parts(key):
    shape = (LANGS, D)
    outer = 1.0 + 0.1 * rough(jax.random.fold_in(key, 51), shape)
    common = rough(jax.random.fold_in(key, 52), shape)
    own = rough(jax.random.fold_in(key, 53), (N_ISLAND,) + shape)
    ramp = 0.1 * (1.0 + 2.0 * jnp.arange(N_ISLAND, dtype=jnp.float32) / max(N_ISLAND - 1, 1))
    local = outer[None] - ramp.reshape(-1, 1, 1) * (common[None] + own)
    return (outer, local)


def draw_outer_gain(key, part):
    return gain_parts(key)[0]


def draw_local_gain(key, part):
    return gain_parts(key)[1].astype(jnp.bfloat16)


def with_ends(values, own_key, low, high):
    longest = values.shape.index(max(values.shape))
    spots = []
    for shift in (0, 1):
        where = [jax.random.randint(jax.random.fold_in(own_key, axis), (), 0, length) for axis, length in enumerate(values.shape)]
        where[longest] = (where[longest] + shift) % values.shape[longest]
        spots.append(tuple(where))
    return values.at[spots[0]].set(low).at[spots[1]].set(high)


def shard_levels(key, extent, shards, least, top_value):
    def one(axis_at, shards_of):
        draws = jax.random.uniform(jax.random.fold_in(jax.random.fold_in(key, 6), axis_at), (shards_of,), jnp.float32, least / len(shards), top_value / len(shards))
        return jnp.repeat(jnp.exp(draws), extent[axis_at] // shards_of).reshape((-1,) + (1,) * (len(extent) - axis_at - 1))

    factor_of = one(*shards[0])
    for cut in shards[1:]:
        factor_of = factor_of * one(*cut)
    return factor_of


def bell_draw(key, dims, deviation, most, pieces=(), held_as=jnp.bfloat16):
    drawn = deviation * jax.random.normal(key, dims, jnp.float32)
    if pieces:
        drawn = drawn * shard_levels(key, dims, pieces, -0.22, 0.18)
    return jnp.clip(drawn, -most, most).astype(held_as)


def setup_inputs(seed: int = 0) -> dict:
    streams_of = jax.random.split(jax.random.key(seed), 12)
    block_input = draw_block_input(jax.random.fold_in(streams_of[11], 71), 0)
    lang_ids = with_ends(jax.random.randint(streams_of[1], (TOKENS,), 0, LANGS), jax.random.fold_in(streams_of[1], 1), 0, LANGS - 1).astype(jnp.int32)
    queries = draw_queries(jax.random.fold_in(streams_of[11], 71), 0)
    saved_keys = draw_saved_keys(jax.random.fold_in(streams_of[11], 71), 0)
    out_grad = draw_out_grad(jax.random.fold_in(streams_of[11], 71), 0)
    local_wv = draw_local_wv(jax.random.fold_in(streams_of[11], 71), 0)
    local_gain = draw_local_gain(jax.random.fold_in(streams_of[11], 71), 0)
    outer_wv = draw_outer_wv(jax.random.fold_in(streams_of[11], 71), 0)
    wv_momentum = bell_draw(streams_of[8], (D, KV_WIDTH), 0.3, 1.8, ((0, 32), (1, 16)), jnp.float32)
    outer_gain = draw_outer_gain(jax.random.fold_in(streams_of[11], 71), 0)
    gain_momentum = bell_draw(streams_of[10], (LANGS, D), 0.3, 1.8, ((0, 16), (1, 32)), jnp.float32)
    return {"block_input": block_input, "lang_ids": lang_ids, "queries": queries, "saved_keys": saved_keys, "out_grad": out_grad, "local_wv": local_wv, "local_gain": local_gain, "outer_wv": outer_wv, "wv_momentum": wv_momentum, "outer_gain": outer_gain, "gain_momentum": gain_momentum}


EPSILON = 1e-05
MOMENTUM = 0.9
OUTER_RATE = 0.7
CLIP_SHARE = 0.25

def normalize(input_rows):
    widened = input_rows.astype(jnp.float32)
    average = lax.optimization_barrier(jnp.mean(widened, axis=-1, keepdims=True))
    centered = widened - average
    variance = lax.optimization_barrier(jnp.mean(centered * centered, axis=-1, keepdims=True))
    return centered * lax.rsqrt(variance + EPSILON)

def value_grad(query_seq, key_seq, grad_seq):
    length = query_seq.shape[0]
    group = HEADS // KV_HEADS
    query_f = query_seq.astype(jnp.float32).reshape(length, KV_HEADS, group, HEAD_DIM)
    key_f = key_seq.astype(jnp.float32).reshape(length, KV_HEADS, HEAD_DIM)
    scores = jnp.einsum('tkgd,skd->kgts', query_f, key_f) * HEAD_DIM ** (-0.5)
    position = jnp.arange(length, dtype=jnp.int32)
    causal = position[:, None] >= position[None, :]
    scores = jnp.where(causal, scores, -jnp.inf)
    row_top = lax.optimization_barrier(jnp.max(scores, axis=-1, keepdims=True))
    exponent = jnp.exp(scores - row_top)
    weights_bf = (exponent / lax.optimization_barrier(jnp.sum(exponent, axis=-1, keepdims=True))).astype(jnp.bfloat16)
    grad_f = grad_seq.astype(jnp.float32).reshape(length, KV_HEADS, group, HEAD_DIM)
    values = jnp.einsum('kgts,tkgd->skd', weights_bf.astype(jnp.float32), grad_f)
    return values.reshape(length, KV_HEADS * HEAD_DIM).astype(jnp.bfloat16)

def island_step(carry, item):
    input_island, lang_island, query_island, key_island, grad_island, wv_island, gain_island = item
    row_count = input_island.shape[0]
    standard = normalize(input_island)
    onehot = (lang_island[None, :] == jnp.arange(LANGS, dtype=jnp.int32)[:, None]).astype(jnp.float32)
    gain_rows = jnp.dot(onehot.T, gain_island.astype(jnp.float32), precision=lax.Precision.HIGHEST)
    normed = (standard * gain_rows).astype(jnp.bfloat16)
    sequences = row_count // SEQ_LEN
    values_grad = lax.map(lambda triple: value_grad(*triple), (query_island.reshape(sequences, SEQ_LEN, -1), key_island.reshape(sequences, SEQ_LEN, -1), grad_island.reshape(sequences, SEQ_LEN, -1)))
    values_grad = values_grad.reshape(row_count, KV_HEADS * HEAD_DIM)
    weight_scale = D ** (-0.5)
    wv_grad = jnp.dot(normed.T, values_grad, preferred_element_type=jnp.float32) * weight_scale
    input_grad = jnp.dot(values_grad, wv_island.T, preferred_element_type=jnp.float32) * weight_scale
    gain_grad = jnp.dot(onehot, standard * input_grad, precision=lax.Precision.HIGHEST)
    wv_norm = jnp.sqrt(jnp.sum(wv_grad * wv_grad))
    gain_norm = jnp.sqrt(jnp.sum(gain_grad * gain_grad))
    wv_clip = jnp.minimum(1.0, CLIP_SHARE * (D * KV_HEADS * HEAD_DIM) ** 0.5 / wv_norm)
    gain_clip = jnp.minimum(1.0, CLIP_SHARE * (LANGS * D) ** 0.5 / gain_norm)
    new_wv = wv_island.astype(jnp.float32) - wv_clip * wv_grad
    new_gain = gain_island.astype(jnp.float32) - gain_clip * gain_grad
    return ((carry[0] + new_wv, carry[1] + new_gain), None)

def reference(block_input, lang_ids, queries, saved_keys, out_grad, local_wv, local_gain, outer_wv, wv_momentum, outer_gain, gain_momentum):
    per_island = TOKENS // N_ISLAND
    items = (block_input.reshape(N_ISLAND, per_island, D), lang_ids.reshape(N_ISLAND, per_island), queries.reshape(N_ISLAND, per_island, -1), saved_keys.reshape(N_ISLAND, per_island, -1), out_grad.reshape(N_ISLAND, per_island, -1), local_wv, local_gain)
    start = (jnp.zeros((D, KV_HEADS * HEAD_DIM), jnp.float32), jnp.zeros((LANGS, D), jnp.float32))
    (sum_wv, sum_gain), _ = lax.scan(island_step, start, items)
    delta_wv = outer_wv - sum_wv / N_ISLAND
    momentum_wv = MOMENTUM * wv_momentum + delta_wv
    result_wv = outer_wv - OUTER_RATE * (delta_wv + MOMENTUM * momentum_wv)
    delta_gain = outer_gain - sum_gain / N_ISLAND
    momentum_gain = MOMENTUM * gain_momentum + delta_gain
    result_gain = outer_gain - OUTER_RATE * (delta_gain + MOMENTUM * momentum_gain)
    return (result_wv, momentum_wv, result_gain, momentum_gain)
```

```python
import jax
import jax.numpy as jnp
from jax import lax
from jax.sharding import PartitionSpec as P

HEADS = 32
KV_HEADS = 4
HEAD_DIM = 128


EPSILON = 1e-05
MOMENTUM = 0.9
OUTER_RATE = 0.7
CLIP_SHARE = 0.25


def row_stats(input_rows):
    widened = input_rows.astype(jnp.float32)
    average = jnp.mean(widened, axis=-1)
    centered = widened - average[:, None]
    variance = jnp.mean(centered * centered, axis=-1)
    return average, lax.rsqrt(variance + EPSILON)


def value_grad(query_rows, key_block, grad_rows):
    length = query_rows.shape[0]
    group = HEADS // KV_HEADS
    query_four = query_rows.reshape(length, KV_HEADS, group, HEAD_DIM)
    key_three = key_block.reshape(length, KV_HEADS, HEAD_DIM)
    scores = jnp.einsum(
        "tkgd,skd->kgts", query_four, key_three, preferred_element_type=jnp.float32
    ) * HEAD_DIM ** (-0.5)
    position = jnp.arange(length, dtype=jnp.int32)
    causal = position[:, None] >= position[None, :]
    scores = jnp.where(causal, scores, -jnp.inf)
    row_top = jnp.max(scores, axis=-1, keepdims=True)
    exponent = jnp.exp(scores - row_top)
    weights_bf = (exponent / jnp.sum(exponent, axis=-1, keepdims=True)).astype(jnp.bfloat16)
    grad_four = grad_rows.reshape(length, KV_HEADS, group, HEAD_DIM)
    values = jnp.einsum("kgts,tkgd->skd", weights_bf, grad_four, preferred_element_type=jnp.float32)
    return values.reshape(length, KV_HEADS * HEAD_DIM).astype(jnp.bfloat16)


def body(
    block_input,
    lang_ids,
    queries,
    saved_keys,
    out_grad,
    local_wv,
    local_gain,
    outer_wv,
    wv_momentum,
    outer_gain,
    gain_momentum,
):
    width = block_input.shape[1]
    fsdp_count = lax.axis_size("fsdp")
    island_count = lax.axis_size("island")
    col_block = width // fsdp_count
    kv_width = local_wv.shape[2]
    lang_count = local_gain.shape[1]
    weight_scale = width ** (-0.5)
    col_begin = lax.axis_index("fsdp") * col_block

    average, inv_std = row_stats(block_input)
    stats = jnp.stack([average, inv_std, lang_ids.astype(jnp.float32)])
    all_stats = lax.all_gather(stats, "fsdp", axis=1, tiled=True)
    col_input = lax.all_to_all(block_input, "fsdp", split_axis=1, concat_axis=0, tiled=True)

    values_grad = value_grad(queries, saved_keys, out_grad)
    all_values = lax.all_gather(values_grad, "fsdp", axis=0, tiled=True)

    standard = (col_input.astype(jnp.float32) - all_stats[0][:, None]) * all_stats[1][:, None]
    all_lang = all_stats[2].astype(jnp.int32)
    lang_table = all_lang[None, :] == jnp.arange(lang_count, dtype=jnp.int32)[:, None]
    own_gain = lax.dynamic_slice_in_dim(local_gain[0], col_begin, col_block, 1)
    gain_rows = jnp.dot(
        lang_table.astype(jnp.bfloat16).T, own_gain, preferred_element_type=jnp.float32
    )
    normed = (standard * gain_rows).astype(jnp.bfloat16)
    weight_rows = local_wv[0]
    input_grad = (
        jnp.dot(all_values, weight_rows.T, preferred_element_type=jnp.float32) * weight_scale
    )
    gain_grad = jnp.dot(
        lang_table.astype(jnp.float32), standard * input_grad, precision=lax.Precision.HIGHEST
    )
    wv_grad = jnp.dot(normed.T, all_values, preferred_element_type=jnp.float32) * weight_scale
    squares = lax.psum(jnp.stack([jnp.sum(wv_grad * wv_grad), jnp.sum(gain_grad * gain_grad)]), "fsdp")
    wv_clip = jnp.minimum(1.0, CLIP_SHARE * (width * kv_width) ** 0.5 / jnp.sqrt(squares[0]))
    gain_clip = jnp.minimum(1.0, CLIP_SHARE * (lang_count * width) ** 0.5 / jnp.sqrt(squares[1]))
    new_wv = weight_rows.astype(jnp.float32) - wv_clip * wv_grad
    new_gain = own_gain.astype(jnp.float32) - gain_clip * gain_grad

    wv_share = kv_width // island_count
    gain_share = lang_count // island_count
    wv_part = new_wv.reshape(col_block, island_count, wv_share).transpose(1, 0, 2)
    wv_part = wv_part.reshape(island_count, col_block * wv_share)
    gain_part = new_gain.reshape(island_count, gain_share * col_block)
    packed = jnp.concatenate([wv_part, gain_part], axis=1)
    total = lax.psum_scatter(packed, "island", scatter_dimension=0, tiled=True)
    total_wv = total[0, : col_block * wv_share].reshape(col_block, wv_share)
    total_gain = total[0, col_block * wv_share :].reshape(gain_share, col_block)

    delta_wv = outer_wv - total_wv / island_count
    momentum_wv = MOMENTUM * wv_momentum + delta_wv
    result_wv = outer_wv - OUTER_RATE * (delta_wv + MOMENTUM * momentum_wv)
    delta_gain = outer_gain - total_gain / island_count
    momentum_gain = MOMENTUM * gain_momentum + delta_gain
    result_gain = outer_gain - OUTER_RATE * (delta_gain + MOMENTUM * momentum_gain)
    return (result_wv, momentum_wv, result_gain, momentum_gain)


def solution(mesh):
    in_specs = (
        P(("island", "fsdp"), None),
        P(("island", "fsdp")),
        P(("island", "fsdp"), None),
        P(("island", "fsdp"), None),
        P(("island", "fsdp"), None),
        P("island", "fsdp", None),
        P("island", None, None),
        P("fsdp", "island"),
        P("fsdp", "island"),
        P("island", "fsdp"),
        P("island", "fsdp"),
    )
    out_specs = (P("fsdp", "island"), P("fsdp", "island"), P("island", "fsdp"), P("island", "fsdp"))
    return jax.shard_map(body, mesh=mesh, in_specs=in_specs, out_specs=out_specs, check_vma=False)
```

```python
import jax
import jax.numpy as jnp
from jax import lax
from jax.sharding import PartitionSpec as P

HEADS = 32
KV_HEADS = 4
HEAD_DIM = 128


EPSILON = 1e-05
MOMENTUM = 0.9
OUTER_RATE = 0.7
CLIP_SHARE = 0.25


def row_stats(input_rows):
    widened = input_rows.astype(jnp.float32)
    average = jnp.mean(widened, axis=-1)
    centered = widened - average[:, None]
    variance = jnp.mean(centered * centered, axis=-1)
    return average, lax.rsqrt(variance + EPSILON)


def value_grad(query_rows, key_block, grad_rows):
    length = query_rows.shape[0]
    group = HEADS // KV_HEADS
    query_four = query_rows.reshape(length, KV_HEADS, group, HEAD_DIM)
    key_three = key_block.reshape(length, KV_HEADS, HEAD_DIM)
    scores = jnp.einsum(
        "tkgd,skd->kgts", query_four, key_three, preferred_element_type=jnp.float32
    ) * HEAD_DIM ** (-0.5)
    position = jnp.arange(length, dtype=jnp.int32)
    causal = position[:, None] >= position[None, :]
    scores = jnp.where(causal, scores, -jnp.inf)
    row_top = jnp.max(scores, axis=-1, keepdims=True)
    exponent = jnp.exp(scores - row_top)
    weights_bf = (exponent / jnp.sum(exponent, axis=-1, keepdims=True)).astype(jnp.bfloat16)
    grad_four = grad_rows.reshape(length, KV_HEADS, group, HEAD_DIM)
    values = jnp.einsum("kgts,tkgd->skd", weights_bf, grad_four, preferred_element_type=jnp.float32)
    return values.reshape(length, KV_HEADS * HEAD_DIM).astype(jnp.bfloat16)


def exchange_sum(part, axis, mask):
    count = lax.axis_size(axis)
    pairs = [(rank, rank ^ mask) for rank in range(count)]
    return part + lax.ppermute(part, axis, pairs)


def doubling_sum(value, axis):
    count = lax.axis_size(axis)
    mask = 1
    while mask < count:
        value = exchange_sum(value, axis, mask)
        mask *= 2
    return value


def halving_scatter(rows, axis, bit_order):
    count = lax.axis_size(axis)
    bits = len(bit_order)
    rank = lax.axis_index(axis)
    grid = rows.reshape((2,) * bits + rows.shape[1:])
    place = list(range(bits))
    for bit in bit_order:
        axis_at = place.index(bit)
        mine = (rank >> (bits - 1 - bit)) & 1
        keep = lax.dynamic_index_in_dim(grid, mine, axis=axis_at, keepdims=False)
        send = lax.dynamic_index_in_dim(grid, 1 - mine, axis=axis_at, keepdims=False)
        mask = 1 << (bits - 1 - bit)
        pairs = [(member, member ^ mask) for member in range(count)]
        grid = keep + lax.ppermute(send, axis, pairs)
        place.pop(axis_at)
    return grid


def body(
    block_input,
    lang_ids,
    queries,
    saved_keys,
    out_grad,
    local_wv,
    local_gain,
    outer_wv,
    wv_momentum,
    outer_gain,
    gain_momentum,
):
    width = block_input.shape[1]
    fsdp_count = lax.axis_size("fsdp")
    island_count = lax.axis_size("island")
    col_block = width // fsdp_count
    kv_width = local_wv.shape[2]
    lang_count = local_gain.shape[1]
    weight_scale = width ** (-0.5)
    col_begin = lax.axis_index("fsdp") * col_block

    average, inv_std = row_stats(block_input)
    stats = jnp.stack([average, inv_std, lang_ids.astype(jnp.float32)])
    all_stats = lax.all_gather(stats, "fsdp", axis=1, tiled=True)
    col_input = lax.all_to_all(block_input, "fsdp", split_axis=1, concat_axis=0, tiled=True)

    values_grad = value_grad(queries, saved_keys, out_grad)
    all_values = lax.all_gather(values_grad, "fsdp", axis=0, tiled=True)

    standard = (col_input.astype(jnp.float32) - all_stats[0][:, None]) * all_stats[1][:, None]
    all_lang = all_stats[2].astype(jnp.int32)
    lang_table = all_lang[None, :] == jnp.arange(lang_count, dtype=jnp.int32)[:, None]
    own_gain = lax.dynamic_slice_in_dim(local_gain[0], col_begin, col_block, 1)
    gain_rows = jnp.dot(
        lang_table.astype(jnp.bfloat16).T, own_gain, preferred_element_type=jnp.float32
    )
    normed = (standard * gain_rows).astype(jnp.bfloat16)
    weight_rows = local_wv[0]
    input_grad = (
        jnp.dot(all_values, weight_rows.T, preferred_element_type=jnp.float32) * weight_scale
    )
    gain_grad = jnp.dot(
        lang_table.astype(jnp.float32), standard * input_grad, precision=lax.Precision.HIGHEST
    )
    wv_grad = jnp.dot(normed.T, all_values, preferred_element_type=jnp.float32) * weight_scale
    squares = doubling_sum(
        jnp.stack([jnp.sum(wv_grad * wv_grad), jnp.sum(gain_grad * gain_grad)]), "fsdp"
    )
    wv_clip = jnp.minimum(1.0, CLIP_SHARE * (width * kv_width) ** 0.5 / jnp.sqrt(squares[0]))
    gain_clip = jnp.minimum(1.0, CLIP_SHARE * (lang_count * width) ** 0.5 / jnp.sqrt(squares[1]))
    new_wv = weight_rows.astype(jnp.float32) - wv_clip * wv_grad
    new_gain = own_gain.astype(jnp.float32) - gain_clip * gain_grad

    wv_share = kv_width // island_count
    gain_share = lang_count // island_count
    wv_part = new_wv.reshape(col_block, island_count, wv_share).transpose(1, 0, 2)
    wv_part = wv_part.reshape(island_count, col_block * wv_share)
    gain_part = new_gain.reshape(island_count, gain_share * col_block)
    packed = jnp.concatenate([wv_part, gain_part], axis=1)
    total = halving_scatter(packed, "island", (2, 1, 3, 0))[None, :]
    total_wv = total[0, : col_block * wv_share].reshape(col_block, wv_share)
    total_gain = total[0, col_block * wv_share :].reshape(gain_share, col_block)

    delta_wv = outer_wv - total_wv / island_count
    momentum_wv = MOMENTUM * wv_momentum + delta_wv
    result_wv = outer_wv - OUTER_RATE * (delta_wv + MOMENTUM * momentum_wv)
    delta_gain = outer_gain - total_gain / island_count
    momentum_gain = MOMENTUM * gain_momentum + delta_gain
    result_gain = outer_gain - OUTER_RATE * (delta_gain + MOMENTUM * momentum_gain)
    return (result_wv, momentum_wv, result_gain, momentum_gain)


def solution(mesh):
    in_specs = (
        P(("island", "fsdp"), None),
        P(("island", "fsdp")),
        P(("island", "fsdp"), None),
        P(("island", "fsdp"), None),
        P(("island", "fsdp"), None),
        P("island", "fsdp", None),
        P("island", None, None),
        P("fsdp", "island"),
        P("fsdp", "island"),
        P("island", "fsdp"),
        P("island", "fsdp"),
    )
    out_specs = (P("fsdp", "island"), P("fsdp", "island"), P("island", "fsdp"), P("island", "fsdp"))
    return jax.shard_map(body, mesh=mesh, in_specs=in_specs, out_specs=out_specs, check_vma=False)
```

```python
import jax
import jax.numpy as jnp
from jax import lax
from jax.sharding import PartitionSpec as P

HEADS = 32
KV_HEADS = 4
HEAD_DIM = 128


EPSILON = 1e-05
MOMENTUM = 0.9
OUTER_RATE = 0.7
CLIP_SHARE = 0.25


def row_stats(input_rows):
    widened = input_rows.astype(jnp.float32)
    average = jnp.mean(widened, axis=-1)
    centered = widened - average[:, None]
    variance = jnp.mean(centered * centered, axis=-1)
    return average, lax.rsqrt(variance + EPSILON)


def value_grad(query_rows, key_block, grad_rows):
    length = query_rows.shape[0]
    group = HEADS // KV_HEADS
    query_four = query_rows.reshape(length, KV_HEADS, group, HEAD_DIM)
    key_three = key_block.reshape(length, KV_HEADS, HEAD_DIM)
    scores = jnp.einsum(
        "tkgd,skd->kgts", query_four, key_three, preferred_element_type=jnp.float32
    ) * HEAD_DIM ** (-0.5)
    position = jnp.arange(length, dtype=jnp.int32)
    causal = position[:, None] >= position[None, :]
    scores = jnp.where(causal, scores, -jnp.inf)
    row_top = jnp.max(scores, axis=-1, keepdims=True)
    exponent = jnp.exp(scores - row_top)
    weights_bf = (exponent / jnp.sum(exponent, axis=-1, keepdims=True)).astype(jnp.bfloat16)
    grad_four = grad_rows.reshape(length, KV_HEADS, group, HEAD_DIM)
    values = jnp.einsum("kgts,tkgd->skd", weights_bf, grad_four, preferred_element_type=jnp.float32)
    return values.reshape(length, KV_HEADS * HEAD_DIM).astype(jnp.bfloat16)


def direct_sum(value, axis):
    count = lax.axis_size(axis)
    rank = lax.axis_index(axis)
    arrived = [value]
    for shift in range(1, count):
        pairs = [(member, (member + shift) % count) for member in range(count)]
        arrived.append(lax.ppermute(value, axis, pairs))
    stacked = jnp.stack(arrived)
    source_order = (rank - jnp.arange(count, dtype=jnp.int32)) % count
    return jnp.sum(jnp.take(stacked, source_order, axis=0), axis=0)


def direct_scatter(rows, axis):
    count = lax.axis_size(axis)
    rank = lax.axis_index(axis)
    arrived = [lax.dynamic_index_in_dim(rows, rank, axis=0, keepdims=False)]
    for shift in range(1, count):
        pairs = [(member, (member + shift) % count) for member in range(count)]
        outgoing = lax.dynamic_index_in_dim(rows, (rank + shift) % count, axis=0, keepdims=False)
        arrived.append(lax.ppermute(outgoing, axis, pairs))
    return jnp.sum(jnp.stack(arrived), axis=0)


def body(
    block_input,
    lang_ids,
    queries,
    saved_keys,
    out_grad,
    local_wv,
    local_gain,
    outer_wv,
    wv_momentum,
    outer_gain,
    gain_momentum,
):
    width = block_input.shape[1]
    fsdp_count = lax.axis_size("fsdp")
    island_count = lax.axis_size("island")
    col_block = width // fsdp_count
    kv_width = local_wv.shape[2]
    lang_count = local_gain.shape[1]
    weight_scale = width ** (-0.5)
    col_begin = lax.axis_index("fsdp") * col_block

    average, inv_std = row_stats(block_input)
    stats = jnp.stack([average, inv_std, lang_ids.astype(jnp.float32)])
    all_stats = lax.all_gather(stats, "fsdp", axis=1, tiled=True)
    col_input = lax.all_to_all(block_input, "fsdp", split_axis=1, concat_axis=0, tiled=True)

    values_grad = value_grad(queries, saved_keys, out_grad)
    all_values = lax.all_gather(values_grad, "fsdp", axis=0, tiled=True)

    standard = (col_input.astype(jnp.float32) - all_stats[0][:, None]) * all_stats[1][:, None]
    all_lang = all_stats[2].astype(jnp.int32)
    lang_table = all_lang[None, :] == jnp.arange(lang_count, dtype=jnp.int32)[:, None]
    own_gain = lax.dynamic_slice_in_dim(local_gain[0], col_begin, col_block, 1)
    gain_rows = jnp.dot(
        lang_table.astype(jnp.bfloat16).T, own_gain, preferred_element_type=jnp.float32
    )
    normed = (standard * gain_rows).astype(jnp.bfloat16)
    weight_rows = local_wv[0]
    input_grad = (
        jnp.dot(all_values, weight_rows.T, preferred_element_type=jnp.float32) * weight_scale
    )
    gain_grad = jnp.dot(
        lang_table.astype(jnp.float32), standard * input_grad, precision=lax.Precision.HIGHEST
    )
    wv_grad = jnp.dot(normed.T, all_values, preferred_element_type=jnp.float32) * weight_scale
    squares = direct_sum(
        jnp.stack([jnp.sum(wv_grad * wv_grad), jnp.sum(gain_grad * gain_grad)]), "fsdp"
    )
    wv_clip = jnp.minimum(1.0, CLIP_SHARE * (width * kv_width) ** 0.5 / jnp.sqrt(squares[0]))
    gain_clip = jnp.minimum(1.0, CLIP_SHARE * (lang_count * width) ** 0.5 / jnp.sqrt(squares[1]))
    new_wv = weight_rows.astype(jnp.float32) - wv_clip * wv_grad
    new_gain = own_gain.astype(jnp.float32) - gain_clip * gain_grad

    wv_share = kv_width // island_count
    gain_share = lang_count // island_count
    wv_part = new_wv.reshape(col_block, island_count, wv_share).transpose(1, 0, 2)
    wv_part = wv_part.reshape(island_count, col_block * wv_share)
    gain_part = new_gain.reshape(island_count, gain_share * col_block)
    packed = jnp.concatenate([wv_part, gain_part], axis=1)
    total = direct_scatter(packed, "island")[None, :]
    total_wv = total[0, : col_block * wv_share].reshape(col_block, wv_share)
    total_gain = total[0, col_block * wv_share :].reshape(gain_share, col_block)

    delta_wv = outer_wv - total_wv / island_count
    momentum_wv = MOMENTUM * wv_momentum + delta_wv
    result_wv = outer_wv - OUTER_RATE * (delta_wv + MOMENTUM * momentum_wv)
    delta_gain = outer_gain - total_gain / island_count
    momentum_gain = MOMENTUM * gain_momentum + delta_gain
    result_gain = outer_gain - OUTER_RATE * (delta_gain + MOMENTUM * momentum_gain)
    return (result_wv, momentum_wv, result_gain, momentum_gain)


def solution(mesh):
    in_specs = (
        P(("island", "fsdp"), None),
        P(("island", "fsdp")),
        P(("island", "fsdp"), None),
        P(("island", "fsdp"), None),
        P(("island", "fsdp"), None),
        P("island", "fsdp", None),
        P("island", None, None),
        P("fsdp", "island"),
        P("fsdp", "island"),
        P("island", "fsdp"),
        P("island", "fsdp"),
    )
    out_specs = (P("fsdp", "island"), P("fsdp", "island"), P("island", "fsdp"), P("island", "fsdp"))
    return jax.shard_map(body, mesh=mesh, in_specs=in_specs, out_specs=out_specs, check_vma=False)
```

```python
import jax
import jax.numpy as jnp
from jax import lax
from jax.sharding import PartitionSpec as P

HEADS = 32
KV_HEADS = 4
HEAD_DIM = 128


EPSILON = 1e-05
MOMENTUM = 0.9
OUTER_RATE = 0.7
CLIP_SHARE = 0.25


def row_stats(input_rows):
    widened = input_rows.astype(jnp.float32)
    average = jnp.mean(widened, axis=-1)
    centered = widened - average[:, None]
    variance = jnp.mean(centered * centered, axis=-1)
    return average, lax.rsqrt(variance + EPSILON)


def value_grad(query_rows, key_block, grad_rows):
    length = query_rows.shape[0]
    group = HEADS // KV_HEADS
    query_four = query_rows.reshape(length, KV_HEADS, group, HEAD_DIM)
    key_three = key_block.reshape(length, KV_HEADS, HEAD_DIM)
    scores = jnp.einsum(
        "tkgd,skd->kgts", query_four, key_three, preferred_element_type=jnp.float32
    ) * HEAD_DIM ** (-0.5)
    position = jnp.arange(length, dtype=jnp.int32)
    causal = position[:, None] >= position[None, :]
    scores = jnp.where(causal, scores, -jnp.inf)
    row_top = jnp.max(scores, axis=-1, keepdims=True)
    exponent = jnp.exp(scores - row_top)
    weights_bf = (exponent / jnp.sum(exponent, axis=-1, keepdims=True)).astype(jnp.bfloat16)
    grad_four = grad_rows.reshape(length, KV_HEADS, group, HEAD_DIM)
    values = jnp.einsum("kgts,tkgd->skd", weights_bf, grad_four, preferred_element_type=jnp.float32)
    return values.reshape(length, KV_HEADS * HEAD_DIM).astype(jnp.bfloat16)


def exchange_sum(part, axis, mask):
    count = lax.axis_size(axis)
    pairs = [(rank, rank ^ mask) for rank in range(count)]
    return part + lax.ppermute(part, axis, pairs)


def doubling_sum(value, axis):
    count = lax.axis_size(axis)
    mask = 1
    while mask < count:
        value = exchange_sum(value, axis, mask)
        mask *= 2
    return value


def halving_scatter(rows, axis, bit_order):
    count = lax.axis_size(axis)
    bits = len(bit_order)
    rank = lax.axis_index(axis)
    grid = rows.reshape((2,) * bits + rows.shape[1:])
    place = list(range(bits))
    for bit in bit_order:
        axis_at = place.index(bit)
        mine = (rank >> (bits - 1 - bit)) & 1
        keep = lax.dynamic_index_in_dim(grid, mine, axis=axis_at, keepdims=False)
        send = lax.dynamic_index_in_dim(grid, 1 - mine, axis=axis_at, keepdims=False)
        mask = 1 << (bits - 1 - bit)
        pairs = [(member, member ^ mask) for member in range(count)]
        grid = keep + lax.ppermute(send, axis, pairs)
        place.pop(axis_at)
    return grid


def split_three(value):
    high = lax.reduce_precision(value, exponent_bits=8, mantissa_bits=7)
    rest = value - high
    middle = lax.reduce_precision(rest, exponent_bits=8, mantissa_bits=7)
    low = rest - middle
    return [part.astype(jnp.bfloat16) for part in (high, middle, low)]


def body(
    block_input,
    lang_ids,
    queries,
    saved_keys,
    out_grad,
    local_wv,
    local_gain,
    outer_wv,
    wv_momentum,
    outer_gain,
    gain_momentum,
):
    width = block_input.shape[1]
    fsdp_count = lax.axis_size("fsdp")
    island_count = lax.axis_size("island")
    col_block = width // fsdp_count
    kv_width = local_wv.shape[2]
    lang_count = local_gain.shape[1]
    weight_scale = width ** (-0.5)
    col_begin = lax.axis_index("fsdp") * col_block

    rows = block_input.shape[0]
    average, inv_std = row_stats(block_input)
    parts = split_three(average) + split_three(inv_std) + [lang_ids.astype(jnp.bfloat16)]
    stat_rows = -(-len(parts) * rows // col_block)
    flat = jnp.concatenate(parts)
    flat = jnp.pad(flat, (0, stat_rows * col_block - flat.shape[0]))
    extra = jnp.broadcast_to(flat.reshape(stat_rows, 1, col_block), (stat_rows, fsdp_count, col_block))
    outgoing = jnp.concatenate([block_input.reshape(rows, fsdp_count, col_block), extra], axis=0)
    arrived = lax.all_to_all(outgoing, "fsdp", split_axis=1, concat_axis=0, tiled=True)
    arrived = arrived.reshape(fsdp_count, rows + stat_rows, col_block)
    col_input = arrived[:, :rows, :].reshape(fsdp_count * rows, col_block)
    got = arrived[:, rows:, :].reshape(fsdp_count, stat_rows * col_block)[:, : len(parts) * rows]
    got = got.reshape(fsdp_count, len(parts), rows).astype(jnp.float32)
    all_average = ((got[:, 0] + got[:, 1]) + got[:, 2]).reshape(-1)
    all_inv_std = ((got[:, 3] + got[:, 4]) + got[:, 5]).reshape(-1)
    all_lang = got[:, 6].reshape(-1).astype(jnp.int32)

    values_grad = value_grad(queries, saved_keys, out_grad)
    all_values = lax.all_gather(values_grad, "fsdp", axis=0, tiled=True)

    standard = (col_input.astype(jnp.float32) - all_average[:, None]) * all_inv_std[:, None]
    lang_table = all_lang[None, :] == jnp.arange(lang_count, dtype=jnp.int32)[:, None]
    own_gain = lax.dynamic_slice_in_dim(local_gain[0], col_begin, col_block, 1)
    gain_rows = jnp.dot(
        lang_table.astype(jnp.bfloat16).T, own_gain, preferred_element_type=jnp.float32
    )
    normed = (standard * gain_rows).astype(jnp.bfloat16)
    weight_rows = local_wv[0]
    input_grad = (
        jnp.dot(all_values, weight_rows.T, preferred_element_type=jnp.float32) * weight_scale
    )
    gain_grad = jnp.dot(
        lang_table.astype(jnp.float32), standard * input_grad, precision=lax.Precision.HIGHEST
    )
    wv_grad = jnp.dot(normed.T, all_values, preferred_element_type=jnp.float32) * weight_scale
    squares = doubling_sum(
        jnp.stack([jnp.sum(wv_grad * wv_grad), jnp.sum(gain_grad * gain_grad)]), "fsdp"
    )
    wv_clip = jnp.minimum(1.0, CLIP_SHARE * (width * kv_width) ** 0.5 / jnp.sqrt(squares[0]))
    gain_clip = jnp.minimum(1.0, CLIP_SHARE * (lang_count * width) ** 0.5 / jnp.sqrt(squares[1]))
    new_wv = weight_rows.astype(jnp.float32) - wv_clip * wv_grad
    new_gain = own_gain.astype(jnp.float32) - gain_clip * gain_grad

    wv_share = kv_width // island_count
    gain_share = lang_count // island_count
    wv_part = new_wv.reshape(col_block, island_count, wv_share).transpose(1, 0, 2)
    wv_part = wv_part.reshape(island_count, col_block * wv_share)
    gain_part = new_gain.reshape(island_count, gain_share * col_block)
    packed = jnp.concatenate([wv_part, gain_part], axis=1)
    total = halving_scatter(packed, "island", (2, 1, 3, 0))[None, :]
    total_wv = total[0, : col_block * wv_share].reshape(col_block, wv_share)
    total_gain = total[0, col_block * wv_share :].reshape(gain_share, col_block)

    delta_wv = outer_wv - total_wv / island_count
    momentum_wv = MOMENTUM * wv_momentum + delta_wv
    result_wv = outer_wv - OUTER_RATE * (delta_wv + MOMENTUM * momentum_wv)
    delta_gain = outer_gain - total_gain / island_count
    momentum_gain = MOMENTUM * gain_momentum + delta_gain
    result_gain = outer_gain - OUTER_RATE * (delta_gain + MOMENTUM * momentum_gain)
    return (result_wv, momentum_wv, result_gain, momentum_gain)


def solution(mesh):
    in_specs = (
        P(("island", "fsdp"), None),
        P(("island", "fsdp")),
        P(("island", "fsdp"), None),
        P(("island", "fsdp"), None),
        P(("island", "fsdp"), None),
        P("island", "fsdp", None),
        P("island", None, None),
        P("fsdp", "island"),
        P("fsdp", "island"),
        P("island", "fsdp"),
        P("island", "fsdp"),
    )
    out_specs = (P("fsdp", "island"), P("fsdp", "island"), P("island", "fsdp"), P("island", "fsdp"))
    return jax.shard_map(body, mesh=mesh, in_specs=in_specs, out_specs=out_specs, check_vma=False)
```

```python
import jax
import jax.numpy as jnp
from jax import lax
from jax.sharding import Mesh, PartitionSpec as P

HEADS = 32
KV_HEADS = 4
HEAD_DIM = 128


EPSILON = 1e-05
MOMENTUM = 0.9
OUTER_RATE = 0.7
CLIP_SHARE = 0.25


def row_stats(input_rows):
    widened = input_rows.astype(jnp.float32)
    average = jnp.mean(widened, axis=-1)
    centered = widened - average[:, None]
    variance = jnp.mean(centered * centered, axis=-1)
    return average, lax.rsqrt(variance + EPSILON)


def value_grad(query_rows, key_block, grad_rows):
    length = query_rows.shape[0]
    group = HEADS // KV_HEADS
    query_four = query_rows.reshape(length, KV_HEADS, group, HEAD_DIM)
    key_three = key_block.reshape(length, KV_HEADS, HEAD_DIM)
    scores = jnp.einsum(
        "tkgd,skd->kgts", query_four, key_three, preferred_element_type=jnp.float32
    ) * HEAD_DIM ** (-0.5)
    position = jnp.arange(length, dtype=jnp.int32)
    causal = position[:, None] >= position[None, :]
    scores = jnp.where(causal, scores, -jnp.inf)
    row_top = jnp.max(scores, axis=-1, keepdims=True)
    exponent = jnp.exp(scores - row_top)
    weights_bf = (exponent / jnp.sum(exponent, axis=-1, keepdims=True)).astype(jnp.bfloat16)
    grad_four = grad_rows.reshape(length, KV_HEADS, group, HEAD_DIM)
    values = jnp.einsum("kgts,tkgd->skd", weights_bf, grad_four, preferred_element_type=jnp.float32)
    return values.reshape(length, KV_HEADS * HEAD_DIM).astype(jnp.bfloat16)


def exchange_sum(part, axis, mask):
    count = lax.axis_size(axis)
    pairs = [(rank, rank ^ mask) for rank in range(count)]
    return part + lax.ppermute(part, axis, pairs)


def doubling_sum(value, axis):
    count = lax.axis_size(axis)
    mask = 1
    while mask < count:
        value = exchange_sum(value, axis, mask)
        mask *= 2
    return value


def halving_scatter(rows, axis, bit_order):
    count = lax.axis_size(axis)
    bits = len(bit_order)
    rank = lax.axis_index(axis)
    grid = rows.reshape((2,) * bits + rows.shape[1:])
    place = list(range(bits))
    for bit in bit_order:
        axis_at = place.index(bit)
        mine = (rank >> (bits - 1 - bit)) & 1
        keep = lax.dynamic_index_in_dim(grid, mine, axis=axis_at, keepdims=False)
        send = lax.dynamic_index_in_dim(grid, 1 - mine, axis=axis_at, keepdims=False)
        mask = 1 << (bits - 1 - bit)
        pairs = [(member, member ^ mask) for member in range(count)]
        grid = keep + lax.ppermute(send, axis, pairs)
        place.pop(axis_at)
    return grid


def split_three(value):
    high = lax.reduce_precision(value, exponent_bits=8, mantissa_bits=7)
    rest = value - high
    middle = lax.reduce_precision(rest, exponent_bits=8, mantissa_bits=7)
    low = rest - middle
    return [part.astype(jnp.bfloat16) for part in (high, middle, low)]


def body(
    block_input,
    lang_ids,
    queries,
    saved_keys,
    out_grad,
    local_wv,
    local_gain,
    outer_wv,
    wv_momentum,
    outer_gain,
    gain_momentum,
):
    width = block_input.shape[1]
    fsdp_count = lax.axis_size("chip") * lax.axis_size("core")
    core = lax.axis_index("core")
    fsdp_at = lax.axis_index("chip") * lax.axis_size("core") + core
    island_count = lax.axis_size("island")
    col_block = width // fsdp_count
    kv_width = local_wv.shape[2]
    lang_count = local_gain.shape[1]
    weight_scale = width ** (-0.5)
    col_begin = fsdp_at * col_block

    rows = block_input.shape[0]
    average, inv_std = row_stats(block_input)
    parts = split_three(average) + split_three(inv_std) + [lang_ids.astype(jnp.bfloat16)]
    stat_rows = -(-len(parts) * rows // col_block)
    flat = jnp.concatenate(parts)
    flat = jnp.pad(flat, (0, stat_rows * col_block - flat.shape[0]))
    extra = jnp.broadcast_to(flat.reshape(stat_rows, 1, col_block), (stat_rows, fsdp_count, col_block))
    outgoing = jnp.concatenate([block_input.reshape(rows, fsdp_count, col_block), extra], axis=0)
    arrived = lax.all_to_all(outgoing, FSDP, split_axis=1, concat_axis=0, tiled=True)
    arrived = arrived.reshape(fsdp_count, rows + stat_rows, col_block)
    col_input = arrived[:, :rows, :].reshape(fsdp_count * rows, col_block)
    got = arrived[:, rows:, :].reshape(fsdp_count, stat_rows * col_block)[:, : len(parts) * rows]
    got = got.reshape(fsdp_count, len(parts), rows).astype(jnp.float32)
    all_average = ((got[:, 0] + got[:, 1]) + got[:, 2]).reshape(-1)
    all_inv_std = ((got[:, 3] + got[:, 4]) + got[:, 5]).reshape(-1)
    all_lang = got[:, 6].reshape(-1).astype(jnp.int32)

    values_grad = value_grad(queries, saved_keys, out_grad)
    own_half = lax.all_gather(values_grad, "chip", axis=0, tiled=True)
    other_half = lax.ppermute(own_half, "core", [(0, 1), (1, 0)])
    first = lax.select(core == 0, own_half, other_half)
    second = lax.select(core == 0, other_half, own_half)
    chips = lax.axis_size("chip")
    all_values = jnp.stack(
        [first.reshape(chips, rows, kv_width), second.reshape(chips, rows, kv_width)], axis=1
    ).reshape(fsdp_count * rows, kv_width)

    standard = (col_input.astype(jnp.float32) - all_average[:, None]) * all_inv_std[:, None]
    lang_table = all_lang[None, :] == jnp.arange(lang_count, dtype=jnp.int32)[:, None]
    own_gain = lax.dynamic_slice_in_dim(local_gain[0], col_begin, col_block, 1)
    gain_rows = jnp.dot(
        lang_table.astype(jnp.bfloat16).T, own_gain, preferred_element_type=jnp.float32
    )
    normed = (standard * gain_rows).astype(jnp.bfloat16)
    weight_rows = local_wv[0]
    input_grad = (
        jnp.dot(all_values, weight_rows.T, preferred_element_type=jnp.float32) * weight_scale
    )
    gain_grad = jnp.dot(
        lang_table.astype(jnp.float32), standard * input_grad, precision=lax.Precision.HIGHEST
    )
    wv_grad = jnp.dot(normed.T, all_values, preferred_element_type=jnp.float32) * weight_scale
    squares = doubling_sum(
        doubling_sum(jnp.stack([jnp.sum(wv_grad * wv_grad), jnp.sum(gain_grad * gain_grad)]), "core"),
        "chip",
    )
    wv_clip = jnp.minimum(1.0, CLIP_SHARE * (width * kv_width) ** 0.5 / jnp.sqrt(squares[0]))
    gain_clip = jnp.minimum(1.0, CLIP_SHARE * (lang_count * width) ** 0.5 / jnp.sqrt(squares[1]))
    new_wv = weight_rows.astype(jnp.float32) - wv_clip * wv_grad
    new_gain = own_gain.astype(jnp.float32) - gain_clip * gain_grad

    wv_share = kv_width // island_count
    gain_share = lang_count // island_count
    wv_part = new_wv.reshape(col_block, island_count, wv_share).transpose(1, 0, 2)
    wv_part = wv_part.reshape(island_count, col_block * wv_share)
    gain_part = new_gain.reshape(island_count, gain_share * col_block)
    packed = jnp.concatenate([wv_part, gain_part], axis=1)
    total = halving_scatter(packed, "island", (2, 1, 3, 0))[None, :]
    total_wv = total[0, : col_block * wv_share].reshape(col_block, wv_share)
    total_gain = total[0, col_block * wv_share :].reshape(gain_share, col_block)

    delta_wv = outer_wv - total_wv / island_count
    momentum_wv = MOMENTUM * wv_momentum + delta_wv
    result_wv = outer_wv - OUTER_RATE * (delta_wv + MOMENTUM * momentum_wv)
    delta_gain = outer_gain - total_gain / island_count
    momentum_gain = MOMENTUM * gain_momentum + delta_gain
    result_gain = outer_gain - OUTER_RATE * (delta_gain + MOMENTUM * momentum_gain)
    return (result_wv, momentum_wv, result_gain, momentum_gain)


FSDP = ("chip", "core")


def solution(mesh):
    island_count, fsdp_count = mesh.devices.shape
    split = Mesh(mesh.devices.reshape(island_count, fsdp_count // 2, 2), ("island", "chip", "core"))
    in_specs = (
        P(("island",) + FSDP, None),
        P(("island",) + FSDP),
        P(("island",) + FSDP, None),
        P(("island",) + FSDP, None),
        P(("island",) + FSDP, None),
        P("island", FSDP, None),
        P("island", None, None),
        P(FSDP, "island"),
        P(FSDP, "island"),
        P("island", FSDP),
        P("island", FSDP),
    )
    out_specs = (P(FSDP, "island"), P(FSDP, "island"), P("island", FSDP), P("island", FSDP))
    return jax.shard_map(body, mesh=split, in_specs=in_specs, out_specs=out_specs, check_vma=False)
```

```python
import jax
import jax.numpy as jnp
from jax import lax
from jax.sharding import PartitionSpec as P

HEADS = 32
KV_HEADS = 4
HEAD_DIM = 128


EPSILON = 1e-05
MOMENTUM = 0.9
OUTER_RATE = 0.7
CLIP_SHARE = 0.25


def row_stats(input_rows):
    widened = input_rows.astype(jnp.float32)
    average = jnp.mean(widened, axis=-1)
    centered = widened - average[:, None]
    variance = jnp.mean(centered * centered, axis=-1)
    return average, lax.rsqrt(variance + EPSILON)


def value_grad(query_rows, key_block, grad_rows):
    length = query_rows.shape[0]
    group = HEADS // KV_HEADS
    query_four = query_rows.reshape(length, KV_HEADS, group, HEAD_DIM)
    key_three = key_block.reshape(length, KV_HEADS, HEAD_DIM)
    scores = jnp.einsum(
        "tkgd,skd->kgts", query_four, key_three, preferred_element_type=jnp.float32
    ) * HEAD_DIM ** (-0.5)
    position = jnp.arange(length, dtype=jnp.int32)
    causal = position[:, None] >= position[None, :]
    scores = jnp.where(causal, scores, -jnp.inf)
    row_top = jnp.max(scores, axis=-1, keepdims=True)
    exponent = jnp.exp(scores - row_top)
    weights_bf = (exponent / jnp.sum(exponent, axis=-1, keepdims=True)).astype(jnp.bfloat16)
    grad_four = grad_rows.reshape(length, KV_HEADS, group, HEAD_DIM)
    values = jnp.einsum("kgts,tkgd->skd", weights_bf, grad_four, preferred_element_type=jnp.float32)
    return values.reshape(length, KV_HEADS * HEAD_DIM).astype(jnp.bfloat16)


def exchange_sum(part, axis, mask):
    count = lax.axis_size(axis)
    pairs = [(rank, rank ^ mask) for rank in range(count)]
    return part + lax.ppermute(part, axis, pairs)


def doubling_sum(value, axis):
    count = lax.axis_size(axis)
    mask = 1
    while mask < count:
        value = exchange_sum(value, axis, mask)
        mask *= 2
    return value


def halving_scatter(rows, axis, bit_order):
    count = lax.axis_size(axis)
    bits = len(bit_order)
    rank = lax.axis_index(axis)
    grid = rows.reshape((2,) * bits + rows.shape[1:])
    place = list(range(bits))
    for bit in bit_order:
        axis_at = place.index(bit)
        mine = (rank >> (bits - 1 - bit)) & 1
        keep = lax.dynamic_index_in_dim(grid, mine, axis=axis_at, keepdims=False)
        send = lax.dynamic_index_in_dim(grid, 1 - mine, axis=axis_at, keepdims=False)
        mask = 1 << (bits - 1 - bit)
        pairs = [(member, member ^ mask) for member in range(count)]
        grid = keep + lax.ppermute(send, axis, pairs)
        place.pop(axis_at)
    return grid


def split_three(value):
    high = lax.reduce_precision(value, exponent_bits=8, mantissa_bits=7)
    rest = value - high
    middle = lax.reduce_precision(rest, exponent_bits=8, mantissa_bits=7)
    low = rest - middle
    return [part.astype(jnp.bfloat16) for part in (high, middle, low)]


def body(
    block_input,
    lang_ids,
    queries,
    saved_keys,
    out_grad,
    local_wv,
    local_gain,
    outer_wv,
    wv_momentum,
    outer_gain,
    gain_momentum,
):
    width = block_input.shape[1]
    fsdp_count = lax.axis_size("fsdp")
    island_count = lax.axis_size("island")
    col_block = width // fsdp_count
    kv_width = local_wv.shape[2]
    lang_count = local_gain.shape[1]
    weight_scale = width ** (-0.5)
    col_begin = lax.axis_index("fsdp") * col_block

    rows = block_input.shape[0]
    average, inv_std = row_stats(block_input)
    parts = split_three(average) + split_three(inv_std) + [lang_ids.astype(jnp.bfloat16)]
    stat_rows = -(-len(parts) * rows // col_block)
    flat = jnp.concatenate(parts)
    flat = jnp.pad(flat, (0, stat_rows * col_block - flat.shape[0]))
    extra = jnp.broadcast_to(flat.reshape(stat_rows, 1, col_block), (stat_rows, fsdp_count, col_block))
    outgoing = jnp.concatenate([block_input.reshape(rows, fsdp_count, col_block), extra], axis=0)

    values_grad = value_grad(queries, saved_keys, out_grad)
    all_values = lax.all_gather(values_grad, "fsdp", axis=0, tiled=True)
    all_values, outgoing = lax.optimization_barrier((all_values, outgoing))
    arrived = lax.all_to_all(outgoing, "fsdp", split_axis=1, concat_axis=0, tiled=True)
    arrived = arrived.reshape(fsdp_count, rows + stat_rows, col_block)
    col_input = arrived[:, :rows, :].reshape(fsdp_count * rows, col_block)
    got = arrived[:, rows:, :].reshape(fsdp_count, stat_rows * col_block)[:, : len(parts) * rows]
    got = got.reshape(fsdp_count, len(parts), rows).astype(jnp.float32)
    all_average = ((got[:, 0] + got[:, 1]) + got[:, 2]).reshape(-1)
    all_inv_std = ((got[:, 3] + got[:, 4]) + got[:, 5]).reshape(-1)
    all_lang = got[:, 6].reshape(-1).astype(jnp.int32)


    standard = (col_input.astype(jnp.float32) - all_average[:, None]) * all_inv_std[:, None]
    lang_table = all_lang[None, :] == jnp.arange(lang_count, dtype=jnp.int32)[:, None]
    own_gain = lax.dynamic_slice_in_dim(local_gain[0], col_begin, col_block, 1)
    gain_rows = jnp.dot(
        lang_table.astype(jnp.bfloat16).T, own_gain, preferred_element_type=jnp.float32
    )
    normed = (standard * gain_rows).astype(jnp.bfloat16)
    weight_rows = local_wv[0]
    input_grad = (
        jnp.dot(all_values, weight_rows.T, preferred_element_type=jnp.float32) * weight_scale
    )
    gain_grad = jnp.dot(
        lang_table.astype(jnp.float32), standard * input_grad, precision=lax.Precision.HIGHEST
    )
    wv_grad = jnp.dot(normed.T, all_values, preferred_element_type=jnp.float32) * weight_scale
    squares = doubling_sum(
        jnp.stack([jnp.sum(wv_grad * wv_grad), jnp.sum(gain_grad * gain_grad)]), "fsdp"
    )
    wv_clip = jnp.minimum(1.0, CLIP_SHARE * (width * kv_width) ** 0.5 / jnp.sqrt(squares[0]))
    gain_clip = jnp.minimum(1.0, CLIP_SHARE * (lang_count * width) ** 0.5 / jnp.sqrt(squares[1]))
    new_wv = weight_rows.astype(jnp.float32) - wv_clip * wv_grad
    new_gain = own_gain.astype(jnp.float32) - gain_clip * gain_grad

    wv_share = kv_width // island_count
    gain_share = lang_count // island_count
    wv_part = new_wv.reshape(col_block, island_count, wv_share).transpose(1, 0, 2)
    wv_part = wv_part.reshape(island_count, col_block * wv_share)
    gain_part = new_gain.reshape(island_count, gain_share * col_block)
    packed = jnp.concatenate([wv_part, gain_part], axis=1)
    total = halving_scatter(packed, "island", (2, 1, 3, 0))[None, :]
    total_wv = total[0, : col_block * wv_share].reshape(col_block, wv_share)
    total_gain = total[0, col_block * wv_share :].reshape(gain_share, col_block)

    delta_wv = outer_wv - total_wv / island_count
    momentum_wv = MOMENTUM * wv_momentum + delta_wv
    result_wv = outer_wv - OUTER_RATE * (delta_wv + MOMENTUM * momentum_wv)
    delta_gain = outer_gain - total_gain / island_count
    momentum_gain = MOMENTUM * gain_momentum + delta_gain
    result_gain = outer_gain - OUTER_RATE * (delta_gain + MOMENTUM * momentum_gain)
    return (result_wv, momentum_wv, result_gain, momentum_gain)


def solution(mesh):
    in_specs = (
        P(("island", "fsdp"), None),
        P(("island", "fsdp")),
        P(("island", "fsdp"), None),
        P(("island", "fsdp"), None),
        P(("island", "fsdp"), None),
        P("island", "fsdp", None),
        P("island", None, None),
        P("fsdp", "island"),
        P("fsdp", "island"),
        P("island", "fsdp"),
        P("island", "fsdp"),
    )
    out_specs = (P("fsdp", "island"), P("fsdp", "island"), P("island", "fsdp"), P("island", "fsdp"))
    return jax.shard_map(body, mesh=mesh, in_specs=in_specs, out_specs=out_specs, check_vma=False)
```

```python
import jax
import jax.numpy as jnp
from jax import lax
from jax.sharding import PartitionSpec as P

HEADS = 32
KV_HEADS = 4
HEAD_DIM = 128


EPSILON = 1e-05
MOMENTUM = 0.9
OUTER_RATE = 0.7
CLIP_SHARE = 0.25


def row_stats(input_rows):
    widened = input_rows.astype(jnp.float32)
    average = jnp.mean(widened, axis=-1)
    centered = widened - average[:, None]
    variance = jnp.mean(centered * centered, axis=-1)
    return average, lax.rsqrt(variance + EPSILON)


def value_grad(query_rows, key_block, grad_rows):
    length = query_rows.shape[0]
    group = HEADS // KV_HEADS
    query_four = query_rows.reshape(length, KV_HEADS, group, HEAD_DIM)
    key_three = key_block.reshape(length, KV_HEADS, HEAD_DIM)
    scores = jnp.einsum(
        "tkgd,skd->kgts", query_four, key_three, preferred_element_type=jnp.float32
    ) * HEAD_DIM ** (-0.5)
    position = jnp.arange(length, dtype=jnp.int32)
    causal = position[:, None] >= position[None, :]
    scores = jnp.where(causal, scores, -jnp.inf)
    row_top = jnp.max(scores, axis=-1, keepdims=True)
    exponent = jnp.exp(scores - row_top)
    weights_bf = (exponent / jnp.sum(exponent, axis=-1, keepdims=True)).astype(jnp.bfloat16)
    grad_four = grad_rows.reshape(length, KV_HEADS, group, HEAD_DIM)
    values = jnp.einsum("kgts,tkgd->skd", weights_bf, grad_four, preferred_element_type=jnp.float32)
    return values.reshape(length, KV_HEADS * HEAD_DIM).astype(jnp.bfloat16)


def exchange_sum(part, axis, mask):
    count = lax.axis_size(axis)
    pairs = [(rank, rank ^ mask) for rank in range(count)]
    return part + lax.ppermute(part, axis, pairs)


def doubling_sum(value, axis):
    count = lax.axis_size(axis)
    mask = 1
    while mask < count:
        value = exchange_sum(value, axis, mask)
        mask *= 2
    return value


def halving_scatter(rows, axis, bit_order):
    count = lax.axis_size(axis)
    bits = len(bit_order)
    rank = lax.axis_index(axis)
    grid = rows.reshape((2,) * bits + rows.shape[1:])
    place = list(range(bits))
    for bit in bit_order:
        axis_at = place.index(bit)
        mine = (rank >> (bits - 1 - bit)) & 1
        keep = lax.dynamic_index_in_dim(grid, mine, axis=axis_at, keepdims=False)
        send = lax.dynamic_index_in_dim(grid, 1 - mine, axis=axis_at, keepdims=False)
        mask = 1 << (bits - 1 - bit)
        pairs = [(member, member ^ mask) for member in range(count)]
        grid = keep + lax.ppermute(send, axis, pairs)
        place.pop(axis_at)
    return grid


def split_three(value):
    high = lax.reduce_precision(value, exponent_bits=8, mantissa_bits=7)
    rest = value - high
    middle = lax.reduce_precision(rest, exponent_bits=8, mantissa_bits=7)
    low = rest - middle
    return [part.astype(jnp.bfloat16) for part in (high, middle, low)]


def body(
    block_input,
    lang_ids,
    queries,
    saved_keys,
    out_grad,
    local_wv,
    local_gain,
    outer_wv,
    wv_momentum,
    outer_gain,
    gain_momentum,
):
    width = block_input.shape[1]
    fsdp_count = lax.axis_size("fsdp")
    island_count = lax.axis_size("island")
    col_block = width // fsdp_count
    kv_width = local_wv.shape[2]
    lang_count = local_gain.shape[1]
    weight_scale = width ** (-0.5)
    col_begin = lax.axis_index("fsdp") * col_block

    rows = block_input.shape[0]
    average, inv_std = row_stats(block_input)
    parts = split_three(average) + split_three(inv_std) + [lang_ids.astype(jnp.bfloat16)]
    stat_rows = -(-len(parts) * rows // col_block)
    flat = jnp.concatenate(parts)
    flat = jnp.pad(flat, (0, stat_rows * col_block - flat.shape[0]))
    extra = jnp.broadcast_to(flat.reshape(stat_rows, 1, col_block), (stat_rows, fsdp_count, col_block))
    outgoing = jnp.concatenate([block_input.reshape(rows, fsdp_count, col_block), extra], axis=0)
    arrived = lax.all_to_all(outgoing, "fsdp", split_axis=1, concat_axis=0, tiled=True)
    arrived = arrived.reshape(fsdp_count, rows + stat_rows, col_block)
    col_input = arrived[:, :rows, :].reshape(fsdp_count * rows, col_block)
    got = arrived[:, rows:, :].reshape(fsdp_count, stat_rows * col_block)[:, : len(parts) * rows]
    got = got.reshape(fsdp_count, len(parts), rows).astype(jnp.float32)
    all_average = ((got[:, 0] + got[:, 1]) + got[:, 2]).reshape(-1)
    all_inv_std = ((got[:, 3] + got[:, 4]) + got[:, 5]).reshape(-1)
    all_lang = got[:, 6].reshape(-1).astype(jnp.int32)

    values_grad = value_grad(queries, saved_keys, out_grad)
    all_values = lax.all_gather(values_grad[None], "fsdp", axis=0, tiled=True)
    all_values = all_values.reshape(fsdp_count * values_grad.shape[0], kv_width)

    standard = (col_input.astype(jnp.float32) - all_average[:, None]) * all_inv_std[:, None]
    lang_table = all_lang[None, :] == jnp.arange(lang_count, dtype=jnp.int32)[:, None]
    own_gain = lax.dynamic_slice_in_dim(local_gain[0], col_begin, col_block, 1)
    gain_rows = jnp.dot(
        lang_table.astype(jnp.bfloat16).T, own_gain, preferred_element_type=jnp.float32
    )
    normed = (standard * gain_rows).astype(jnp.bfloat16)
    weight_rows = local_wv[0]
    input_grad = (
        jnp.dot(all_values, weight_rows.T, preferred_element_type=jnp.float32) * weight_scale
    )
    gain_grad = jnp.dot(
        lang_table.astype(jnp.float32), standard * input_grad, precision=lax.Precision.HIGHEST
    )
    wv_grad = jnp.dot(normed.T, all_values, preferred_element_type=jnp.float32) * weight_scale
    squares = doubling_sum(
        jnp.stack([jnp.sum(wv_grad * wv_grad), jnp.sum(gain_grad * gain_grad)]), "fsdp"
    )
    wv_clip = jnp.minimum(1.0, CLIP_SHARE * (width * kv_width) ** 0.5 / jnp.sqrt(squares[0]))
    gain_clip = jnp.minimum(1.0, CLIP_SHARE * (lang_count * width) ** 0.5 / jnp.sqrt(squares[1]))
    new_wv = weight_rows.astype(jnp.float32) - wv_clip * wv_grad
    new_gain = own_gain.astype(jnp.float32) - gain_clip * gain_grad

    wv_share = kv_width // island_count
    gain_share = lang_count // island_count
    wv_part = new_wv.reshape(col_block, island_count, wv_share).transpose(1, 0, 2)
    wv_part = wv_part.reshape(island_count, col_block * wv_share)
    gain_part = new_gain.reshape(island_count, gain_share * col_block)
    packed = jnp.concatenate([wv_part, gain_part], axis=1)
    total = halving_scatter(packed, "island", (2, 1, 3, 0))[None, :]
    total_wv = total[0, : col_block * wv_share].reshape(col_block, wv_share)
    total_gain = total[0, col_block * wv_share :].reshape(gain_share, col_block)

    delta_wv = outer_wv - total_wv / island_count
    momentum_wv = MOMENTUM * wv_momentum + delta_wv
    result_wv = outer_wv - OUTER_RATE * (delta_wv + MOMENTUM * momentum_wv)
    delta_gain = outer_gain - total_gain / island_count
    momentum_gain = MOMENTUM * gain_momentum + delta_gain
    result_gain = outer_gain - OUTER_RATE * (delta_gain + MOMENTUM * momentum_gain)
    return (result_wv, momentum_wv, result_gain, momentum_gain)


def solution(mesh):
    in_specs = (
        P(("island", "fsdp"), None),
        P(("island", "fsdp")),
        P(("island", "fsdp"), None),
        P(("island", "fsdp"), None),
        P(("island", "fsdp"), None),
        P("island", "fsdp", None),
        P("island", None, None),
        P("fsdp", "island"),
        P("fsdp", "island"),
        P("island", "fsdp"),
        P("island", "fsdp"),
    )
    out_specs = (P("fsdp", "island"), P("fsdp", "island"), P("island", "fsdp"), P("island", "fsdp"))
    return jax.shard_map(body, mesh=mesh, in_specs=in_specs, out_specs=out_specs, check_vma=False)
```

```python
import jax
import jax.numpy as jnp
from jax import lax
from jax.sharding import PartitionSpec as P

HEADS = 32
KV_HEADS = 4
HEAD_DIM = 128


EPSILON = 1e-05
MOMENTUM = 0.9
OUTER_RATE = 0.7
CLIP_SHARE = 0.25


def row_stats(input_rows):
    widened = input_rows.astype(jnp.float32)
    average = jnp.mean(widened, axis=-1)
    centered = widened - average[:, None]
    variance = jnp.mean(centered * centered, axis=-1)
    return average, lax.rsqrt(variance + EPSILON)


def value_grad(query_rows, key_block, grad_rows):
    length = query_rows.shape[0]
    group = HEADS // KV_HEADS
    query_four = query_rows.reshape(length, KV_HEADS, group, HEAD_DIM)
    key_three = key_block.reshape(length, KV_HEADS, HEAD_DIM)
    scores = jnp.einsum(
        "tkgd,skd->kgts", query_four, key_three, preferred_element_type=jnp.float32
    ) * HEAD_DIM ** (-0.5)
    position = jnp.arange(length, dtype=jnp.int32)
    causal = position[:, None] >= position[None, :]
    scores = jnp.where(causal, scores, -jnp.inf)
    row_top = jnp.max(scores, axis=-1, keepdims=True)
    exponent = jnp.exp(scores - row_top)
    weights_bf = (exponent / jnp.sum(exponent, axis=-1, keepdims=True)).astype(jnp.bfloat16)
    grad_four = grad_rows.reshape(length, KV_HEADS, group, HEAD_DIM)
    values = jnp.einsum("kgts,tkgd->skd", weights_bf, grad_four, preferred_element_type=jnp.float32)
    return values.reshape(length, KV_HEADS * HEAD_DIM).astype(jnp.bfloat16)


def exchange_sum(part, axis, mask):
    count = lax.axis_size(axis)
    pairs = [(rank, rank ^ mask) for rank in range(count)]
    return part + lax.ppermute(part, axis, pairs)


def doubling_sum(value, axis):
    count = lax.axis_size(axis)
    mask = 1
    while mask < count:
        value = exchange_sum(value, axis, mask)
        mask *= 2
    return value


def halving_scatter(rows, axis, bit_order):
    count = lax.axis_size(axis)
    bits = len(bit_order)
    rank = lax.axis_index(axis)
    grid = rows.reshape((2,) * bits + rows.shape[1:])
    place = list(range(bits))
    for bit in bit_order:
        axis_at = place.index(bit)
        mine = (rank >> (bits - 1 - bit)) & 1
        keep = lax.dynamic_index_in_dim(grid, mine, axis=axis_at, keepdims=False)
        send = lax.dynamic_index_in_dim(grid, 1 - mine, axis=axis_at, keepdims=False)
        mask = 1 << (bits - 1 - bit)
        pairs = [(member, member ^ mask) for member in range(count)]
        grid = keep + lax.ppermute(send, axis, pairs)
        place.pop(axis_at)
    return grid


def split_three(value):
    high = lax.reduce_precision(value, exponent_bits=8, mantissa_bits=7)
    rest = value - high
    middle = lax.reduce_precision(rest, exponent_bits=8, mantissa_bits=7)
    low = rest - middle
    return [part.astype(jnp.bfloat16) for part in (high, middle, low)]


def body(
    block_input,
    lang_ids,
    queries,
    saved_keys,
    out_grad,
    local_wv,
    local_gain,
    outer_wv,
    wv_momentum,
    outer_gain,
    gain_momentum,
):
    width = block_input.shape[1]
    fsdp_count = lax.axis_size("fsdp")
    island_count = lax.axis_size("island")
    col_block = width // fsdp_count
    kv_width = local_wv.shape[2]
    lang_count = local_gain.shape[1]
    weight_scale = width ** (-0.5)
    col_begin = lax.axis_index("fsdp") * col_block

    rows = block_input.shape[0]
    average, inv_std = row_stats(block_input)
    parts = split_three(average) + split_three(inv_std) + [lang_ids.astype(jnp.bfloat16)]
    stat_rows = -(-len(parts) * rows // kv_width)
    flat = jnp.concatenate(parts)
    flat = jnp.pad(flat, (0, stat_rows * kv_width - flat.shape[0]))
    col_input = lax.all_to_all(block_input, "fsdp", split_axis=1, concat_axis=0, tiled=True)

    values_grad = value_grad(queries, saved_keys, out_grad)
    outgoing = jnp.concatenate([values_grad, flat.reshape(stat_rows, kv_width)], axis=0)
    arrived = lax.all_gather(outgoing[None], "fsdp", axis=0, tiled=True)
    all_values = arrived[:, :rows, :].reshape(fsdp_count * rows, kv_width)
    got = arrived[:, rows:, :].reshape(fsdp_count, stat_rows * kv_width)[:, : len(parts) * rows]
    got = got.reshape(fsdp_count, len(parts), rows).astype(jnp.float32)
    all_average = ((got[:, 0] + got[:, 1]) + got[:, 2]).reshape(-1)
    all_inv_std = ((got[:, 3] + got[:, 4]) + got[:, 5]).reshape(-1)
    all_lang = got[:, 6].reshape(-1).astype(jnp.int32)

    standard = (col_input.astype(jnp.float32) - all_average[:, None]) * all_inv_std[:, None]
    lang_table = all_lang[None, :] == jnp.arange(lang_count, dtype=jnp.int32)[:, None]
    own_gain = lax.dynamic_slice_in_dim(local_gain[0], col_begin, col_block, 1)
    gain_rows = jnp.dot(
        lang_table.astype(jnp.bfloat16).T, own_gain, preferred_element_type=jnp.float32
    )
    normed = (standard * gain_rows).astype(jnp.bfloat16)
    weight_rows = local_wv[0]
    input_grad = (
        jnp.dot(all_values, weight_rows.T, preferred_element_type=jnp.float32) * weight_scale
    )
    gain_grad = jnp.dot(
        lang_table.astype(jnp.float32), standard * input_grad, precision=lax.Precision.HIGHEST
    )
    wv_grad = jnp.dot(normed.T, all_values, preferred_element_type=jnp.float32) * weight_scale
    squares = doubling_sum(
        jnp.stack([jnp.sum(wv_grad * wv_grad), jnp.sum(gain_grad * gain_grad)]), "fsdp"
    )
    wv_clip = jnp.minimum(1.0, CLIP_SHARE * (width * kv_width) ** 0.5 / jnp.sqrt(squares[0]))
    gain_clip = jnp.minimum(1.0, CLIP_SHARE * (lang_count * width) ** 0.5 / jnp.sqrt(squares[1]))
    new_wv = weight_rows.astype(jnp.float32) - wv_clip * wv_grad
    new_gain = own_gain.astype(jnp.float32) - gain_clip * gain_grad

    wv_share = kv_width // island_count
    gain_share = lang_count // island_count
    wv_part = new_wv.reshape(col_block, island_count, wv_share).transpose(1, 0, 2)
    wv_part = wv_part.reshape(island_count, col_block * wv_share)
    gain_part = new_gain.reshape(island_count, gain_share * col_block)
    packed = jnp.concatenate([wv_part, gain_part], axis=1)
    total = halving_scatter(packed, "island", (2, 1, 3, 0))[None, :]
    total_wv = total[0, : col_block * wv_share].reshape(col_block, wv_share)
    total_gain = total[0, col_block * wv_share :].reshape(gain_share, col_block)

    delta_wv = outer_wv - total_wv / island_count
    momentum_wv = MOMENTUM * wv_momentum + delta_wv
    result_wv = outer_wv - OUTER_RATE * (delta_wv + MOMENTUM * momentum_wv)
    delta_gain = outer_gain - total_gain / island_count
    momentum_gain = MOMENTUM * gain_momentum + delta_gain
    result_gain = outer_gain - OUTER_RATE * (delta_gain + MOMENTUM * momentum_gain)
    return (result_wv, momentum_wv, result_gain, momentum_gain)


def solution(mesh):
    in_specs = (
        P(("island", "fsdp"), None),
        P(("island", "fsdp")),
        P(("island", "fsdp"), None),
        P(("island", "fsdp"), None),
        P(("island", "fsdp"), None),
        P("island", "fsdp", None),
        P("island", None, None),
        P("fsdp", "island"),
        P("fsdp", "island"),
        P("island", "fsdp"),
        P("island", "fsdp"),
    )
    out_specs = (P("fsdp", "island"), P("fsdp", "island"), P("island", "fsdp"), P("island", "fsdp"))
    return jax.shard_map(body, mesh=mesh, in_specs=in_specs, out_specs=out_specs, check_vma=False)
```

```python
import jax
import jax.numpy as jnp
from jax import lax
from jax.sharding import PartitionSpec as P

HEADS = 32
KV_HEADS = 4
HEAD_DIM = 128


EPSILON = 1e-05
MOMENTUM = 0.9
OUTER_RATE = 0.7
CLIP_SHARE = 0.25


def row_stats(input_rows):
    widened = input_rows.astype(jnp.float32)
    average = jnp.mean(widened, axis=-1)
    centered = widened - average[:, None]
    variance = jnp.mean(centered * centered, axis=-1)
    return average, lax.rsqrt(variance + EPSILON)


def value_grad(query_rows, key_block, grad_rows):
    length = query_rows.shape[0]
    group = HEADS // KV_HEADS
    query_four = query_rows.reshape(length, KV_HEADS, group, HEAD_DIM)
    key_three = key_block.reshape(length, KV_HEADS, HEAD_DIM)
    scores = jnp.einsum(
        "tkgd,skd->kgts", query_four, key_three, preferred_element_type=jnp.float32
    ) * HEAD_DIM ** (-0.5)
    position = jnp.arange(length, dtype=jnp.int32)
    causal = position[:, None] >= position[None, :]
    scores = jnp.where(causal, scores, -jnp.inf)
    row_top = jnp.max(scores, axis=-1, keepdims=True)
    exponent = jnp.exp(scores - row_top)
    weights_bf = (exponent / jnp.sum(exponent, axis=-1, keepdims=True)).astype(jnp.bfloat16)
    grad_four = grad_rows.reshape(length, KV_HEADS, group, HEAD_DIM)
    values = jnp.einsum("kgts,tkgd->skd", weights_bf, grad_four, preferred_element_type=jnp.float32)
    return values.reshape(length, KV_HEADS * HEAD_DIM).astype(jnp.bfloat16)


def exchange_sum(part, axis, mask):
    count = lax.axis_size(axis)
    pairs = [(rank, rank ^ mask) for rank in range(count)]
    return part + lax.ppermute(part, axis, pairs)


def doubling_sum(value, axis):
    count = lax.axis_size(axis)
    mask = 1
    while mask < count:
        value = exchange_sum(value, axis, mask)
        mask *= 2
    return value


def halving_scatter(rows, axis, bit_order):
    count = lax.axis_size(axis)
    bits = len(bit_order)
    rank = lax.axis_index(axis)
    grid = rows.reshape((2,) * bits + rows.shape[1:])
    place = list(range(bits))
    for bit in bit_order:
        axis_at = place.index(bit)
        mine = (rank >> (bits - 1 - bit)) & 1
        keep = lax.dynamic_index_in_dim(grid, mine, axis=axis_at, keepdims=False)
        send = lax.dynamic_index_in_dim(grid, 1 - mine, axis=axis_at, keepdims=False)
        mask = 1 << (bits - 1 - bit)
        pairs = [(member, member ^ mask) for member in range(count)]
        grid = keep + lax.ppermute(send, axis, pairs)
        place.pop(axis_at)
    return grid


def split_three(value):
    high = lax.reduce_precision(value, exponent_bits=8, mantissa_bits=7)
    rest = value - high
    middle = lax.reduce_precision(rest, exponent_bits=8, mantissa_bits=7)
    low = rest - middle
    return [part.astype(jnp.bfloat16) for part in (high, middle, low)]


def body(
    block_input,
    lang_ids,
    queries,
    saved_keys,
    out_grad,
    local_wv,
    local_gain,
    outer_wv,
    wv_momentum,
    outer_gain,
    gain_momentum,
):
    width = block_input.shape[1]
    fsdp_count = lax.axis_size("fsdp")
    island_count = lax.axis_size("island")
    col_block = width // fsdp_count
    kv_width = local_wv.shape[2]
    lang_count = local_gain.shape[1]
    weight_scale = width ** (-0.5)
    col_begin = lax.axis_index("fsdp") * col_block

    rows = block_input.shape[0]
    average, inv_std = row_stats(block_input)
    parts = split_three(average) + split_three(inv_std) + [lang_ids.astype(jnp.bfloat16)]
    stat_rows = -(-len(parts) * rows // col_block)
    flat = jnp.concatenate(parts)
    flat = jnp.pad(flat, (0, stat_rows * col_block - flat.shape[0]))
    extra = jnp.broadcast_to(flat.reshape(stat_rows, 1, col_block), (stat_rows, fsdp_count, col_block))
    outgoing = jnp.concatenate([block_input.reshape(rows, fsdp_count, col_block), extra], axis=0)
    arrived = lax.all_to_all(outgoing, "fsdp", split_axis=1, concat_axis=0, tiled=True)
    arrived = arrived.reshape(fsdp_count, rows + stat_rows, col_block)
    col_input = arrived[:, :rows, :].reshape(fsdp_count * rows, col_block)
    got = arrived[:, rows:, :].reshape(fsdp_count, stat_rows * col_block)[:, : len(parts) * rows]
    got = got.reshape(fsdp_count, len(parts), rows).astype(jnp.float32)
    all_average = ((got[:, 0] + got[:, 1]) + got[:, 2]).reshape(-1)
    all_inv_std = ((got[:, 3] + got[:, 4]) + got[:, 5]).reshape(-1)
    all_lang = got[:, 6].reshape(-1).astype(jnp.int32)

    values_grad = value_grad(queries, saved_keys, out_grad)
    all_values = lax.all_gather(values_grad[None], "fsdp", axis=0, tiled=True)
    all_values = all_values.reshape(fsdp_count * values_grad.shape[0], kv_width)

    standard = (col_input.astype(jnp.float32) - all_average[:, None]) * all_inv_std[:, None]
    lang_table = all_lang[None, :] == jnp.arange(lang_count, dtype=jnp.int32)[:, None]
    own_gain = lax.dynamic_slice_in_dim(local_gain[0], col_begin, col_block, 1)
    gain_rows = jnp.dot(
        lang_table.astype(jnp.bfloat16).T, own_gain, preferred_element_type=jnp.float32
    )
    normed = (standard * gain_rows).astype(jnp.bfloat16)
    weight_rows = local_wv[0]
    input_grad = (
        jnp.dot(all_values, weight_rows.T, preferred_element_type=jnp.float32) * weight_scale
    )
    gain_grad = jnp.dot(
        lang_table.astype(jnp.float32), standard * input_grad, precision=lax.Precision.HIGHEST
    )
    wv_grad = jnp.dot(normed.T, all_values, preferred_element_type=jnp.float32) * weight_scale
    partial = jnp.stack([jnp.sum(wv_grad * wv_grad), jnp.sum(gain_grad * gain_grad)])
    partials = lax.all_to_all(
        jnp.broadcast_to(partial, (fsdp_count, 2)), "fsdp", split_axis=0, concat_axis=0, tiled=True
    )
    squares = jnp.sum(partials, axis=0)
    wv_clip = jnp.minimum(1.0, CLIP_SHARE * (width * kv_width) ** 0.5 / jnp.sqrt(squares[0]))
    gain_clip = jnp.minimum(1.0, CLIP_SHARE * (lang_count * width) ** 0.5 / jnp.sqrt(squares[1]))
    new_wv = weight_rows.astype(jnp.float32) - wv_clip * wv_grad
    new_gain = own_gain.astype(jnp.float32) - gain_clip * gain_grad

    wv_share = kv_width // island_count
    gain_share = lang_count // island_count
    wv_part = new_wv.reshape(col_block, island_count, wv_share).transpose(1, 0, 2)
    wv_part = wv_part.reshape(island_count, col_block * wv_share)
    gain_part = new_gain.reshape(island_count, gain_share * col_block)
    packed = jnp.concatenate([wv_part, gain_part], axis=1)
    total = jnp.sum(
        lax.all_to_all(packed, "island", split_axis=0, concat_axis=0, tiled=True), axis=0, keepdims=True
    )
    total_wv = total[0, : col_block * wv_share].reshape(col_block, wv_share)
    total_gain = total[0, col_block * wv_share :].reshape(gain_share, col_block)

    delta_wv = outer_wv - total_wv / island_count
    momentum_wv = MOMENTUM * wv_momentum + delta_wv
    result_wv = outer_wv - OUTER_RATE * (delta_wv + MOMENTUM * momentum_wv)
    delta_gain = outer_gain - total_gain / island_count
    momentum_gain = MOMENTUM * gain_momentum + delta_gain
    result_gain = outer_gain - OUTER_RATE * (delta_gain + MOMENTUM * momentum_gain)
    return (result_wv, momentum_wv, result_gain, momentum_gain)


def solution(mesh):
    in_specs = (
        P(("island", "fsdp"), None),
        P(("island", "fsdp")),
        P(("island", "fsdp"), None),
        P(("island", "fsdp"), None),
        P(("island", "fsdp"), None),
        P("island", "fsdp", None),
        P("island", None, None),
        P("fsdp", "island"),
        P("fsdp", "island"),
        P("island", "fsdp"),
        P("island", "fsdp"),
    )
    out_specs = (P("fsdp", "island"), P("fsdp", "island"), P("island", "fsdp"), P("island", "fsdp"))
    return jax.shard_map(body, mesh=mesh, in_specs=in_specs, out_specs=out_specs, check_vma=False)
```

```python
import jax
import jax.numpy as jnp
from jax import lax
from jax.sharding import PartitionSpec as P

HEADS = 32
KV_HEADS = 4
HEAD_DIM = 128


EPSILON = 1e-05
MOMENTUM = 0.9
OUTER_RATE = 0.7
CLIP_SHARE = 0.25


def row_stats(input_rows):
    widened = input_rows.astype(jnp.float32)
    average = jnp.mean(widened, axis=-1)
    centered = widened - average[:, None]
    variance = jnp.mean(centered * centered, axis=-1)
    return average, lax.rsqrt(variance + EPSILON)


def value_grad(query_rows, key_block, grad_rows):
    length = query_rows.shape[0]
    group = HEADS // KV_HEADS
    query_four = query_rows.reshape(length, KV_HEADS, group, HEAD_DIM)
    key_three = key_block.reshape(length, KV_HEADS, HEAD_DIM)
    scores = jnp.einsum(
        "tkgd,skd->kgts", query_four, key_three, preferred_element_type=jnp.float32
    ) * HEAD_DIM ** (-0.5)
    position = jnp.arange(length, dtype=jnp.int32)
    causal = position[:, None] >= position[None, :]
    scores = jnp.where(causal, scores, -jnp.inf)
    row_top = jnp.max(scores, axis=-1, keepdims=True)
    exponent = jnp.exp(scores - row_top)
    weights_bf = (exponent / jnp.sum(exponent, axis=-1, keepdims=True)).astype(jnp.bfloat16)
    grad_four = grad_rows.reshape(length, KV_HEADS, group, HEAD_DIM)
    values = jnp.einsum("kgts,tkgd->skd", weights_bf, grad_four, preferred_element_type=jnp.float32)
    return values.reshape(length, KV_HEADS * HEAD_DIM).astype(jnp.bfloat16)


def exchange_sum(part, axis, mask):
    count = lax.axis_size(axis)
    pairs = [(rank, rank ^ mask) for rank in range(count)]
    return part + lax.ppermute(part, axis, pairs)


def doubling_sum(value, axis):
    count = lax.axis_size(axis)
    mask = 1
    while mask < count:
        value = exchange_sum(value, axis, mask)
        mask *= 2
    return value


def halving_scatter(rows, axis, bit_order):
    count = lax.axis_size(axis)
    bits = len(bit_order)
    rank = lax.axis_index(axis)
    grid = rows.reshape((2,) * bits + rows.shape[1:])
    place = list(range(bits))
    for bit in bit_order:
        axis_at = place.index(bit)
        mine = (rank >> (bits - 1 - bit)) & 1
        keep = lax.dynamic_index_in_dim(grid, mine, axis=axis_at, keepdims=False)
        send = lax.dynamic_index_in_dim(grid, 1 - mine, axis=axis_at, keepdims=False)
        mask = 1 << (bits - 1 - bit)
        pairs = [(member, member ^ mask) for member in range(count)]
        grid = keep + lax.ppermute(send, axis, pairs)
        place.pop(axis_at)
    return grid


def split_three(value):
    high = lax.reduce_precision(value, exponent_bits=8, mantissa_bits=7)
    rest = value - high
    middle = lax.reduce_precision(rest, exponent_bits=8, mantissa_bits=7)
    low = rest - middle
    return [part.astype(jnp.bfloat16) for part in (high, middle, low)]


def body(
    block_input,
    lang_ids,
    queries,
    saved_keys,
    out_grad,
    local_wv,
    local_gain,
    outer_wv,
    wv_momentum,
    outer_gain,
    gain_momentum,
):
    width = block_input.shape[1]
    fsdp_count = lax.axis_size("fsdp")
    island_count = lax.axis_size("island")
    col_block = width // fsdp_count
    kv_width = local_wv.shape[2]
    lang_count = local_gain.shape[1]
    weight_scale = width ** (-0.5)
    col_begin = lax.axis_index("fsdp") * col_block

    rows = block_input.shape[0]
    average, inv_std = row_stats(block_input)
    parts = split_three(average) + split_three(inv_std) + [lang_ids.astype(jnp.bfloat16)]
    stat_rows = -(-len(parts) * rows // col_block)
    flat = jnp.concatenate(parts)
    flat = jnp.pad(flat, (0, stat_rows * col_block - flat.shape[0]))
    extra = jnp.broadcast_to(flat.reshape(1, stat_rows, col_block), (fsdp_count, stat_rows, col_block))
    columns = block_input.reshape(rows, fsdp_count, col_block).transpose(1, 0, 2)
    outgoing = jnp.concatenate([columns, extra], axis=1)
    arrived = lax.all_to_all(outgoing, "fsdp", split_axis=0, concat_axis=0, tiled=True)
    col_input = arrived[:, :rows, :].reshape(fsdp_count * rows, col_block)
    got = arrived[:, rows:, :].reshape(fsdp_count, stat_rows * col_block)[:, : len(parts) * rows]
    got = got.reshape(fsdp_count, len(parts), rows).astype(jnp.float32)
    all_average = ((got[:, 0] + got[:, 1]) + got[:, 2]).reshape(-1)
    all_inv_std = ((got[:, 3] + got[:, 4]) + got[:, 5]).reshape(-1)
    all_lang = got[:, 6].reshape(-1).astype(jnp.int32)

    values_grad = value_grad(queries, saved_keys, out_grad)
    all_values = lax.all_gather(values_grad[None], "fsdp", axis=0, tiled=True)
    all_values = all_values.reshape(fsdp_count * values_grad.shape[0], kv_width)

    standard = (col_input.astype(jnp.float32) - all_average[:, None]) * all_inv_std[:, None]
    lang_table = all_lang[None, :] == jnp.arange(lang_count, dtype=jnp.int32)[:, None]
    own_gain = lax.dynamic_slice_in_dim(local_gain[0], col_begin, col_block, 1)
    gain_rows = jnp.dot(
        lang_table.astype(jnp.bfloat16).T, own_gain, preferred_element_type=jnp.float32
    )
    normed = (standard * gain_rows).astype(jnp.bfloat16)
    weight_rows = local_wv[0]
    input_grad = (
        jnp.dot(all_values, weight_rows.T, preferred_element_type=jnp.float32) * weight_scale
    )
    gain_grad = jnp.dot(
        lang_table.astype(jnp.float32), standard * input_grad, precision=lax.Precision.HIGHEST
    )
    wv_grad = jnp.dot(normed.T, all_values, preferred_element_type=jnp.float32) * weight_scale
    partial = jnp.stack([jnp.sum(wv_grad * wv_grad), jnp.sum(gain_grad * gain_grad)])
    partials = lax.all_to_all(
        jnp.broadcast_to(partial, (fsdp_count, 2)), "fsdp", split_axis=0, concat_axis=0, tiled=True
    )
    squares = jnp.sum(partials, axis=0)
    wv_clip = jnp.minimum(1.0, CLIP_SHARE * (width * kv_width) ** 0.5 / jnp.sqrt(squares[0]))
    gain_clip = jnp.minimum(1.0, CLIP_SHARE * (lang_count * width) ** 0.5 / jnp.sqrt(squares[1]))
    new_wv = weight_rows.astype(jnp.float32) - wv_clip * wv_grad
    new_gain = own_gain.astype(jnp.float32) - gain_clip * gain_grad

    wv_share = kv_width // island_count
    gain_share = lang_count // island_count
    wv_part = new_wv.reshape(col_block, island_count, wv_share).transpose(1, 0, 2)
    wv_part = wv_part.reshape(island_count, col_block * wv_share)
    gain_part = new_gain.reshape(island_count, gain_share * col_block)
    packed = jnp.concatenate([wv_part, gain_part], axis=1)
    total = jnp.sum(
        lax.all_to_all(packed, "island", split_axis=0, concat_axis=0, tiled=True), axis=0, keepdims=True
    )
    total_wv = total[0, : col_block * wv_share].reshape(col_block, wv_share)
    total_gain = total[0, col_block * wv_share :].reshape(gain_share, col_block)

    delta_wv = outer_wv - total_wv / island_count
    momentum_wv = MOMENTUM * wv_momentum + delta_wv
    result_wv = outer_wv - OUTER_RATE * (delta_wv + MOMENTUM * momentum_wv)
    delta_gain = outer_gain - total_gain / island_count
    momentum_gain = MOMENTUM * gain_momentum + delta_gain
    result_gain = outer_gain - OUTER_RATE * (delta_gain + MOMENTUM * momentum_gain)
    return (result_wv, momentum_wv, result_gain, momentum_gain)


def solution(mesh):
    in_specs = (
        P(("island", "fsdp"), None),
        P(("island", "fsdp")),
        P(("island", "fsdp"), None),
        P(("island", "fsdp"), None),
        P(("island", "fsdp"), None),
        P("island", "fsdp", None),
        P("island", None, None),
        P("fsdp", "island"),
        P("fsdp", "island"),
        P("island", "fsdp"),
        P("island", "fsdp"),
    )
    out_specs = (P("fsdp", "island"), P("fsdp", "island"), P("island", "fsdp"), P("island", "fsdp"))
    return jax.shard_map(body, mesh=mesh, in_specs=in_specs, out_specs=out_specs, check_vma=False)
```

```python
import jax
import jax.numpy as jnp
from jax import lax
from jax.sharding import PartitionSpec as P

HEADS = 32
KV_HEADS = 4
HEAD_DIM = 128


EPSILON = 1e-05
MOMENTUM = 0.9
OUTER_RATE = 0.7
CLIP_SHARE = 0.25


def row_stats(input_rows):
    widened = input_rows.astype(jnp.float32)
    average = jnp.mean(widened, axis=-1)
    centered = widened - average[:, None]
    variance = jnp.mean(centered * centered, axis=-1)
    return average, lax.rsqrt(variance + EPSILON)


def value_grad(query_rows, key_block, grad_rows):
    length = query_rows.shape[0]
    group = HEADS // KV_HEADS
    query_four = query_rows.reshape(length, KV_HEADS, group, HEAD_DIM)
    key_three = key_block.reshape(length, KV_HEADS, HEAD_DIM)
    scores = jnp.einsum(
        "tkgd,skd->kgts", query_four, key_three, preferred_element_type=jnp.float32
    ) * HEAD_DIM ** (-0.5)
    position = jnp.arange(length, dtype=jnp.int32)
    causal = position[:, None] >= position[None, :]
    scores = jnp.where(causal, scores, -jnp.inf)
    row_top = jnp.max(scores, axis=-1, keepdims=True)
    exponent = jnp.exp(scores - row_top)
    weights_bf = (exponent / jnp.sum(exponent, axis=-1, keepdims=True)).astype(jnp.bfloat16)
    grad_four = grad_rows.reshape(length, KV_HEADS, group, HEAD_DIM)
    values = jnp.einsum("kgts,tkgd->skd", weights_bf, grad_four, preferred_element_type=jnp.float32)
    return values.reshape(length, KV_HEADS * HEAD_DIM).astype(jnp.bfloat16)


def exchange_sum(part, axis, mask):
    count = lax.axis_size(axis)
    pairs = [(rank, rank ^ mask) for rank in range(count)]
    return part + lax.ppermute(part, axis, pairs)


def doubling_sum(value, axis):
    count = lax.axis_size(axis)
    mask = 1
    while mask < count:
        value = exchange_sum(value, axis, mask)
        mask *= 2
    return value


def halving_scatter(rows, axis, bit_order):
    count = lax.axis_size(axis)
    bits = len(bit_order)
    rank = lax.axis_index(axis)
    grid = rows.reshape((2,) * bits + rows.shape[1:])
    place = list(range(bits))
    for bit in bit_order:
        axis_at = place.index(bit)
        mine = (rank >> (bits - 1 - bit)) & 1
        keep = lax.dynamic_index_in_dim(grid, mine, axis=axis_at, keepdims=False)
        send = lax.dynamic_index_in_dim(grid, 1 - mine, axis=axis_at, keepdims=False)
        mask = 1 << (bits - 1 - bit)
        pairs = [(member, member ^ mask) for member in range(count)]
        grid = keep + lax.ppermute(send, axis, pairs)
        place.pop(axis_at)
    return grid


def split_three(value):
    high = lax.reduce_precision(value, exponent_bits=8, mantissa_bits=7)
    rest = value - high
    middle = lax.reduce_precision(rest, exponent_bits=8, mantissa_bits=7)
    low = rest - middle
    return [part.astype(jnp.bfloat16) for part in (high, middle, low)]


def body(
    block_input,
    lang_ids,
    queries,
    saved_keys,
    out_grad,
    local_wv,
    local_gain,
    outer_wv,
    wv_momentum,
    outer_gain,
    gain_momentum,
):
    width = block_input.shape[1]
    fsdp_count = lax.axis_size("fsdp")
    island_count = lax.axis_size("island")
    col_block = width // fsdp_count
    kv_width = local_wv.shape[2]
    lang_count = local_gain.shape[1]
    weight_scale = width ** (-0.5)
    col_begin = lax.axis_index("fsdp") * col_block

    rows = block_input.shape[0]
    average, inv_std = row_stats(block_input)
    parts = split_three(average) + split_three(inv_std) + [lang_ids.astype(jnp.bfloat16)]
    stat_rows = -(-len(parts) * rows // col_block)
    flat = jnp.concatenate(parts)
    flat = jnp.pad(flat, (0, stat_rows * col_block - flat.shape[0]))
    extra = jnp.broadcast_to(flat.reshape(stat_rows, 1, col_block), (stat_rows, fsdp_count, col_block))
    outgoing = jnp.concatenate([block_input.reshape(rows, fsdp_count, col_block), extra], axis=0)
    arrived = lax.all_to_all(outgoing, "fsdp", split_axis=1, concat_axis=0, tiled=True)
    arrived = arrived.reshape(fsdp_count, rows + stat_rows, col_block)
    col_input = arrived[:, :rows, :].reshape(fsdp_count * rows, col_block)
    got = arrived[:, rows:, :].reshape(fsdp_count, stat_rows * col_block)[:, : len(parts) * rows]
    got = got.reshape(fsdp_count, len(parts), rows).astype(jnp.float32)
    all_average = ((got[:, 0] + got[:, 1]) + got[:, 2]).reshape(-1)
    all_inv_std = ((got[:, 3] + got[:, 4]) + got[:, 5]).reshape(-1)
    all_lang = got[:, 6].reshape(-1).astype(jnp.int32)

    values_grad = value_grad(queries, saved_keys, out_grad)
    all_values = lax.all_gather(values_grad[None], "fsdp", axis=0, tiled=True)
    all_values = all_values.reshape(fsdp_count * values_grad.shape[0], kv_width)

    standard = (col_input.astype(jnp.float32) - all_average[:, None]) * all_inv_std[:, None]
    lang_table = all_lang[None, :] == jnp.arange(lang_count, dtype=jnp.int32)[:, None]
    own_gain = lax.dynamic_slice_in_dim(local_gain[0], col_begin, col_block, 1)
    gain_rows = jnp.dot(
        lang_table.astype(jnp.bfloat16).T, own_gain, preferred_element_type=jnp.float32
    )
    normed = (standard * gain_rows).astype(jnp.bfloat16)
    weight_rows = local_wv[0]
    input_grad = (
        jnp.dot(all_values, weight_rows.T, preferred_element_type=jnp.float32) * weight_scale
    )
    gain_grad = jnp.dot(
        lang_table.astype(jnp.float32), standard * input_grad, precision=lax.Precision.HIGH
    )
    wv_grad = jnp.dot(normed.T, all_values, preferred_element_type=jnp.float32) * weight_scale
    partial = jnp.stack([jnp.sum(wv_grad * wv_grad), jnp.sum(gain_grad * gain_grad)])
    partials = lax.all_to_all(
        jnp.broadcast_to(partial, (fsdp_count, 2)), "fsdp", split_axis=0, concat_axis=0, tiled=True
    )
    squares = jnp.sum(partials, axis=0)
    wv_clip = jnp.minimum(1.0, CLIP_SHARE * (width * kv_width) ** 0.5 / jnp.sqrt(squares[0]))
    gain_clip = jnp.minimum(1.0, CLIP_SHARE * (lang_count * width) ** 0.5 / jnp.sqrt(squares[1]))
    new_wv = weight_rows.astype(jnp.float32) - wv_clip * wv_grad
    new_gain = own_gain.astype(jnp.float32) - gain_clip * gain_grad

    wv_share = kv_width // island_count
    gain_share = lang_count // island_count
    wv_part = new_wv.reshape(col_block, island_count, wv_share).transpose(1, 0, 2)
    wv_part = wv_part.reshape(island_count, col_block * wv_share)
    gain_part = new_gain.reshape(island_count, gain_share * col_block)
    packed = jnp.concatenate([wv_part, gain_part], axis=1)
    total = jnp.sum(
        lax.all_to_all(packed, "island", split_axis=0, concat_axis=0, tiled=True), axis=0, keepdims=True
    )
    total_wv = total[0, : col_block * wv_share].reshape(col_block, wv_share)
    total_gain = total[0, col_block * wv_share :].reshape(gain_share, col_block)

    delta_wv = outer_wv - total_wv / island_count
    momentum_wv = MOMENTUM * wv_momentum + delta_wv
    result_wv = outer_wv - OUTER_RATE * (delta_wv + MOMENTUM * momentum_wv)
    delta_gain = outer_gain - total_gain / island_count
    momentum_gain = MOMENTUM * gain_momentum + delta_gain
    result_gain = outer_gain - OUTER_RATE * (delta_gain + MOMENTUM * momentum_gain)
    return (result_wv, momentum_wv, result_gain, momentum_gain)


def solution(mesh):
    in_specs = (
        P(("island", "fsdp"), None),
        P(("island", "fsdp")),
        P(("island", "fsdp"), None),
        P(("island", "fsdp"), None),
        P(("island", "fsdp"), None),
        P("island", "fsdp", None),
        P("island", None, None),
        P("fsdp", "island"),
        P("fsdp", "island"),
        P("island", "fsdp"),
        P("island", "fsdp"),
    )
    out_specs = (P("fsdp", "island"), P("fsdp", "island"), P("island", "fsdp"), P("island", "fsdp"))
    return jax.shard_map(body, mesh=mesh, in_specs=in_specs, out_specs=out_specs, check_vma=False)
```
